256 devices in a mesh: region: 8 (over x, core), dp: 32 (over y, z).
Axes of the slice: x: 4, y: 4, z: 8, core: 2. Of those that a mesh axis runs over, the one named last changes fastest.
Arguments:
- cells: bfloat16 [32, 131072, 256], P('dp', 'region'), may hold values from -12 to 12
- cell_weight: float32 [32, 131072], P('dp', 'region'), may hold values from 0.1 to 10
- cell_cluster: int32 [32, 131072], P('dp', 'region'), may hold values from -1 to 2047, as said below
- cluster_edges: int32 [32, 2048, 8], P('dp', 'region'), may hold values from 0 to 2047, as said below
- labels: int32 [32, 2048], P('dp', 'region'), may hold values from 0 to 7
- w_self: bfloat16 [256, 1024], replicated, may hold values from -0.375 to 0.375
- w_nbr: bfloat16 [256, 1024], replicated, may hold values from -0.375 to 0.375
- w_out: bfloat16 [1024, 8], replicated, may hold values from -0.1875 to 0.1875
Outputs:
- logits: float32 [32, 2048, 8], P('dp', 'region')
- grad_self: float32 [256, 1024], replicated
- grad_nbr: float32 [256, 1024], replicated
- grad_out: float32 [1024, 8], replicated
The draws below stay inside these ranges and needn't reach their ends.
Inputs may be any that keep to these rules, and one draw needn't show every extreme that they name: `cell_cluster`: clusters (r) * 256 to ((r) + 1) * 256 - 1 belong to region r; a cell's cluster belongs to the cell's own region or an adjacent one; every cluster has at least one cell. `cluster_edges`: A cluster's neighbours belong to its own region or an adjacent one; every cluster is listed by some cluster.
All inputs are finite; a program needn't handle non-finite values.
Results may differ from the reference program's by a relative error of at most 0.0051.
Values may be sent and summed in bfloat16 or wider, within the bound.
No kernel may reach another device: no remote copies, remote signals or barrier semaphores. Data moves between devices by JAX's collectives and lax.ppermute only.
A program may use at most 64 MiB of HBM per device.

```python
import math
import jax
import jax.numpy as jnp
from jax import lax

F = 256
HID = 1024
NCLS = 8
DEG = 8
CELL_DEV = 16384
CL_DEV = 256
EVENTS = 32
CELLS = 131072
CLUSTERS = 2048
N_REGION = 8


def draw_cell_cluster(key, part):
    k_order, k_kind, k_side, k_pick = jax.random.split(key, 4)
    shape = (EVENTS, N_REGION, CELL_DEV)
    keys = jax.random.split(k_order, EVENTS * N_REGION)
    order = jax.vmap(lambda k: jax.random.permutation(k, CELL_DEV))(keys).reshape(shape).astype(jnp.int32)
    region = jnp.arange(N_REGION, dtype=jnp.int32)[None, :, None]
    kind = jax.random.randint(k_kind, shape, 0, 20)
    side = jax.random.randint(k_side, shape, 0, 2) * 2 - 1
    pick = jax.random.randint(k_pick, shape, 0, CL_DEV)
    span_cut = 3 + region * 6 // max(N_REGION - 1, 1)
    other = jnp.clip(region + side, 0, N_REGION - 1)
    target = jnp.where(kind < span_cut, other, region)
    random_id = jnp.where(kind < 2, -1, target * CL_DEV + pick)
    ids = jnp.where(order < CL_DEV, region * CL_DEV + order, random_id)
    return ids.reshape(EVENTS, CELLS).astype(jnp.int32)


def draw_cluster_edges(key, part):
    k_order, k_off, k_pick = jax.random.split(key, 3)
    shape = (EVENTS, CLUSTERS, DEG)
    keys = jax.random.split(k_order, EVENTS * N_REGION)
    order = jax.vmap(lambda k: jax.random.permutation(k, CL_DEV))(keys).reshape(EVENTS, CLUSTERS).astype(jnp.int32)
    own = (jnp.arange(CLUSTERS, dtype=jnp.int32) // CL_DEV)[None, :, None]
    offset = jax.random.randint(k_off, shape, 0, 4)
    step = jnp.where(offset == 0, -1, jnp.where(offset == 3, 1, 0))
    target = jnp.clip(own + step, 0, N_REGION - 1)
    edges = target * CL_DEV + jax.random.randint(k_pick, shape, 0, CL_DEV)
    first = own[:, :, 0] * CL_DEV + order
    edges = edges.at[:, :, 0].set(first)
    return edges.astype(jnp.int32)


def with_ends(values, key, smallest, high):
    index_at = [jax.random.randint(jax.random.fold_in(key, axis), (), 0, length) for axis, length in enumerate(values.shape)]
    widest = values.shape.index(max(values.shape))
    next_to = index_at[:widest] + [(index_at[widest] + 1) % values.shape[widest]] + index_at[widest + 1:]
    return values.at[tuple(index_at)].set(smallest).at[tuple(next_to)].set(high)


def block_levels(key, shape, pieces, least, top_value):
    def one(dim, blocks):
        heights = jax.random.uniform(jax.random.fold_in(jax.random.fold_in(key, 6), dim), (blocks,), jnp.float32, least / len(pieces), top_value / len(pieces))
        return jnp.repeat(jnp.exp(heights), shape[dim] // blocks).reshape((-1,) + (1,) * (len(shape) - dim - 1))

    level = one(*pieces[0])
    for cut in pieces[1:]:
        level = level * one(*cut)
    return level


def scatter_about(rng, extent, scale, bound, shards=(), held_as=jnp.bfloat16):
    result = jax.random.normal(rng, extent, jnp.float32) * scale
    if len(shards) > 0:
        result = block_levels(rng, extent, shards, -0.22, 0.18) * result
    return jnp.clip(result, min=-bound, max=bound).astype(held_as)


def setup_inputs(seed: int = 0) -> dict:
    key_of = jax.random.split(jax.random.key(seed), 9)
    cells = scatter_about(key_of[0], (EVENTS, CELLS, F), 2.0, 12.0, ((0, 32), (1, 8)))
    cell_weight = jnp.clip(jnp.exp(math.log(10.0) - 4.6051702 * jax.random.uniform(key_of[1], (EVENTS, CELLS), jnp.float32) ** block_levels(key_of[1], (EVENTS, CELLS), ((0, 32), (1, 8)), -0.2, 0.2)), 0.1, 10.0)
    cell_cluster = draw_cell_cluster(jax.random.fold_in(key_of[8], 71), 0)
    cluster_edges = draw_cluster_edges(jax.random.fold_in(key_of[8], 71), 0)
    labels = with_ends(jax.random.randint(key_of[4], (EVENTS, CLUSTERS), 0, NCLS), jax.random.fold_in(key_of[4], 1), 0, NCLS - 1).astype(jnp.int32)
    w_self = scatter_about(key_of[5], (F, HID), F ** -0.5, 0.375)
    w_nbr = scatter_about(key_of[6], (F, HID), F ** -0.5, 0.375)
    w_out = scatter_about(key_of[7], (HID, NCLS), HID ** -0.5, 0.1875)
    return {"cells": cells, "cell_weight": cell_weight, "cell_cluster": cell_cluster, "cluster_edges": cluster_edges, "labels": labels, "w_self": w_self, "w_nbr": w_nbr, "w_out": w_out}


def reference(cells, cell_weight, cell_cluster, cluster_edges, labels, w_self, w_nbr, w_out):
    def one_event(packed):
        cell_rows, weights, ids, edges, classes = packed
        weighted = (weights[:, None] * cell_rows.astype(jnp.float32)).astype(jnp.bfloat16)
        segments = jnp.where(ids < 0, CLUSTERS, ids).astype(jnp.int32)
        numer = jax.ops.segment_sum(weighted.astype(jnp.float32), segments, CLUSTERS + 1)[:CLUSTERS]
        denom = jax.ops.segment_sum(weights, segments, CLUSTERS + 1)[:CLUSTERS]
        pooled = (numer / denom[:, None]).astype(jnp.bfloat16)
        agg = (jnp.sum(pooled[edges].astype(jnp.float32), axis=1) / DEG).astype(jnp.bfloat16)
        zval = jnp.dot(pooled, w_self, preferred_element_type=jnp.float32) + jnp.dot(agg, w_nbr, preferred_element_type=jnp.float32)
        sig = jax.nn.sigmoid(zval)
        units = (zval * sig).astype(jnp.bfloat16)
        scores = jnp.dot(units, w_out, preferred_element_type=jnp.float32)
        target = (classes[:, None] == jnp.arange(NCLS, dtype=jnp.int32)[None, :]).astype(jnp.float32)
        d_logits = ((jax.nn.sigmoid(scores) - target) / EVENTS).astype(jnp.bfloat16)
        grad_head = jnp.dot(units.T, d_logits, preferred_element_type=jnp.float32)
        d_units = jnp.dot(d_logits, w_out.T, preferred_element_type=jnp.float32)
        d_z = (d_units * sig * (1.0 + zval * (1.0 - sig))).astype(jnp.bfloat16)
        grad_own = jnp.dot(pooled.T, d_z, preferred_element_type=jnp.float32)
        grad_side = jnp.dot(agg.T, d_z, preferred_element_type=jnp.float32)
        return scores, grad_own, grad_side, grad_head

    scores, grad_own, grad_side, grad_head = lax.map(one_event, (cells, cell_weight, cell_cluster, cluster_edges, labels))
    return scores, jnp.sum(grad_own, axis=0), jnp.sum(grad_side, axis=0), jnp.sum(grad_head, axis=0)
```

```python
import jax
import jax.numpy as jnp
from jax import lax
from jax.sharding import PartitionSpec as P


def passed_along(value, axis, steps):
    count = lax.axis_size(axis)
    initial, last = (max(0, -steps), min(count, count - steps))
    return lax.ppermute(value, axis, [(source, source + steps) for source in range(initial, last)])


def padded(block, sides, width):
    for axis, dim in sides:
        count = lax.axis_size(axis)
        forward = [(i, i + 1) for i in range(count - 1)]
        backward = [(target, source) for source, target in forward]
        low = lax.ppermute(
            lax.slice_in_dim(block, block.shape[dim] - width, None, axis=dim), axis, forward
        )
        high = lax.ppermute(lax.slice_in_dim(block, 0, width, axis=dim), axis, backward)
        block = jnp.concatenate([low, block, high], axis=dim)
    return block


def accumulate(cluster_ids, weighted, weights, width):
    events, length, feats = weighted.shape
    block = min(512, length)
    slots = jnp.arange(width, dtype=jnp.int32)

    def add_block(index, carry):
        numer, denom = carry
        start = index * block
        ids = lax.dynamic_slice_in_dim(cluster_ids, start, block, 1)
        rows = lax.dynamic_slice_in_dim(weighted, start, block, 1)
        scale = lax.dynamic_slice_in_dim(weights, start, block, 1)
        member = ids[:, None, :] == slots[None, :, None]
        numer = numer + jnp.einsum(
            "ekb,ebf->ekf", member.astype(jnp.bfloat16), rows, preferred_element_type=jnp.float32
        )
        denom = denom + jnp.einsum(
            "ekb,eb->ek", member.astype(jnp.float32), scale, precision=lax.Precision.HIGHEST
        )
        return (numer, denom)

    start_sums = (
        jnp.zeros((events, width, feats), jnp.float32),
        jnp.zeros((events, width), jnp.float32),
    )
    return lax.fori_loop(0, length // block, add_block, start_sums)


def halving_plan(sizes):
    core = [("region", 1)]
    first = [("region", 2), ("dp", 8), ("dp", 1), ("region", 4), ("dp", 16), ("dp", 2), ("dp", 4)]
    second = [("dp", 8), ("dp", 1), ("region", 2), ("dp", 16), ("dp", 2), ("region", 4), ("dp", 4)]
    width = sizes["dp"]
    steps = []
    for flip0, flip1 in zip(core + first, core + second):
        perm, bits = [], []
        for device in range(sizes["region"] * width):
            at = {"region": device // width, "dp": device % width}
            axis, bit = flip1 if at["region"] & 1 else flip0
            bits.append(1 if at[axis] & bit else 0)
            at[axis] ^= bit
            perm.append((device, at["region"] * width + at["dp"]))
        steps.append((perm, bits))
    return steps


def all_sum(buffers, sizes):
    axes = ("region", "dp")
    me = lax.axis_index("region") * sizes["dp"] + lax.axis_index("dp")
    steps = halving_plan(sizes)
    for perm, bits in steps:
        upper = jnp.asarray(bits, jnp.int32)[me] == 1
        keeps, sends = [], []
        for value in buffers:
            half = value.shape[0] // 2
            low, high = value[:half], value[half:]
            keeps.append(jnp.where(upper, high, low))
            sends.append(jnp.where(upper, low, high))
        got = lax.ppermute(tuple(sends), axes, perm)
        buffers = tuple(k + g for k, g in zip(keeps, got))
    for perm, bits in reversed(steps):
        upper = jnp.asarray(bits, jnp.int32)[me] == 1
        got = lax.ppermute(buffers, axes, perm)
        buffers = tuple(
            jnp.concatenate([jnp.where(upper, g, v), jnp.where(upper, v, g)], axis=0)
            for v, g in zip(buffers, got)
        )
    return buffers


def local(cells, cell_weight, cell_cluster, cluster_edges, labels, w_self, w_nbr, w_out):
    region = lax.axis_index("region")
    owned = cluster_edges.shape[1]
    degree = cluster_edges.shape[2]
    weighted = (cell_weight[..., None] * cells.astype(jnp.float32)).astype(jnp.bfloat16)
    relative = cell_cluster - (region - 1) * owned
    numer_three, denom_three = accumulate(relative, weighted, cell_weight, 3 * owned)
    above_numer, above_denom = passed_along(
        (numer_three[:, :owned], denom_three[:, :owned]), "region", -1
    )
    below_numer, below_denom = passed_along(
        (numer_three[:, 2 * owned :], denom_three[:, 2 * owned :]), "region", 1
    )
    numer = numer_three[:, owned : 2 * owned] + above_numer + below_numer
    denom = denom_three[:, owned : 2 * owned] + above_denom + below_denom
    pooled = (numer / denom[..., None]).astype(jnp.bfloat16)
    table = padded(pooled, (("region", 1),), owned)
    targets = cluster_edges - (region - 1) * owned
    width = 3 * owned
    slots = jnp.arange(width, dtype=jnp.int32)
    tally = jnp.zeros((pooled.shape[0], owned, width), jnp.float32)
    for which in range(degree):
        tally = tally + (targets[:, :, which, None] == slots[None, None, :]).astype(jnp.float32)
    agg = (
        jnp.einsum(
            "ekj,ejf->ekf", tally.astype(jnp.bfloat16), table, preferred_element_type=jnp.float32
        )
        / degree
    ).astype(jnp.bfloat16)
    zval = jnp.einsum("ekf,fh->ekh", pooled, w_self, preferred_element_type=jnp.float32)
    zval = zval + jnp.einsum("ekf,fh->ekh", agg, w_nbr, preferred_element_type=jnp.float32)
    sig = jax.nn.sigmoid(zval)
    units = (zval * sig).astype(jnp.bfloat16)
    scores = jnp.einsum("ekh,hc->ekc", units, w_out, preferred_element_type=jnp.float32)
    events = lax.axis_size("dp") * cells.shape[0]
    classes = jnp.arange(w_out.shape[1], dtype=jnp.int32)
    target = (labels[..., None] == classes[None, None, :]).astype(jnp.float32)
    d_logits = ((jax.nn.sigmoid(scores) - target) / events).astype(jnp.bfloat16)
    grad_head = jnp.einsum("ekh,ekc->ch", units, d_logits, preferred_element_type=jnp.float32)
    d_units = jnp.einsum("ekc,hc->ekh", d_logits, w_out, preferred_element_type=jnp.float32)
    d_z = (d_units * sig * (1.0 + zval * (1.0 - sig))).astype(jnp.bfloat16)
    grad_own = jnp.einsum("ekf,ekh->fh", pooled, d_z, preferred_element_type=jnp.float32)
    grad_side = jnp.einsum("ekf,ekh->fh", agg, d_z, preferred_element_type=jnp.float32)
    sizes = {"region": lax.axis_size("region"), "dp": lax.axis_size("dp")}
    hid = grad_own.shape[1]
    grads, head = all_sum(
        (jnp.concatenate([grad_own, grad_side], axis=0), grad_head.reshape(-1)), sizes
    )
    grad_own, grad_side = grads[: pooled.shape[2]], grads[pooled.shape[2] :]
    grad_head = head.reshape(-1, hid).T
    return (scores, grad_own, grad_side, grad_head)


def solution(mesh):
    return jax.shard_map(
        local,
        mesh=mesh,
        in_specs=(
            P("dp", "region", None),
            P("dp", "region"),
            P("dp", "region"),
            P("dp", "region", None),
            P("dp", "region"),
            P(),
            P(),
            P(),
        ),
        out_specs=(P("dp", "region", None), P(), P(), P()),
        check_vma=False,
    )
```

```python
import jax
import jax.numpy as jnp
from jax import lax
from jax.experimental import pallas as pl
from jax.sharding import PartitionSpec as P


def passed_along(value, axis, steps):
    count = lax.axis_size(axis)
    initial, last = (max(0, -steps), min(count, count - steps))
    return lax.ppermute(value, axis, [(source, source + steps) for source in range(initial, last)])


def padded(block, sides, width):
    for axis, dim in sides:
        count = lax.axis_size(axis)
        forward = [(i, i + 1) for i in range(count - 1)]
        backward = [(target, source) for source, target in forward]
        low = lax.ppermute(
            lax.slice_in_dim(block, block.shape[dim] - width, None, axis=dim), axis, forward
        )
        high = lax.ppermute(lax.slice_in_dim(block, 0, width, axis=dim), axis, backward)
        block = jnp.concatenate([low, block, high], axis=dim)
    return block


def pooled_sums_kernel(ids_ref, rows_ref, sums_ref):
    @pl.when(pl.program_id(0) == 0)
    def _():
        sums_ref[...] = jnp.zeros_like(sums_ref)

    width = sums_ref.shape[0]
    slots = lax.broadcasted_iota(jnp.int32, (width, ids_ref.shape[1]), 0)
    member = (ids_ref[...] == slots).astype(jnp.bfloat16)
    sums_ref[...] += jnp.dot(member, rows_ref[...], preferred_element_type=jnp.float32)


def accumulate(cluster_ids, weighted, weights, width):
    length, feats = weighted.shape
    high = weights.astype(jnp.bfloat16)
    rest = weights - high.astype(jnp.float32)
    middle = rest.astype(jnp.bfloat16)
    low = (rest - middle.astype(jnp.float32)).astype(jnp.bfloat16)
    lanes = 128
    parts = jnp.stack([high, middle, low], axis=-1)
    rows = jnp.concatenate(
        [weighted, parts, jnp.zeros((length, lanes - 3), jnp.bfloat16)], axis=-1
    )
    block = min(1024, length)
    total = feats + lanes
    sums = pl.pallas_call(
        pooled_sums_kernel,
        grid=(length // block,),
        in_specs=[
            pl.BlockSpec((1, block), lambda i: (0, i)),
            pl.BlockSpec((block, total), lambda i: (i, 0)),
        ],
        out_specs=pl.BlockSpec((width, total), lambda i: (0, 0)),
        out_shape=jax.ShapeDtypeStruct((width, total), jnp.float32),
        cost_estimate=pl.CostEstimate(
            flops=2 * width * length * total,
            bytes_accessed=length * total * 2 + length * 4 + width * total * 4,
            transcendentals=0,
        ),
    )(cluster_ids.reshape(1, length), rows)
    numer = sums[:, :feats]
    denom = sums[:, feats] + sums[:, feats + 1] + sums[:, feats + 2]
    return numer[None], denom[None]


def halving_plan(sizes):
    core = [("region", 1)]
    first = [("region", 2), ("dp", 8), ("dp", 1), ("region", 4), ("dp", 16), ("dp", 2), ("dp", 4)]
    second = [("dp", 8), ("dp", 1), ("region", 2), ("dp", 16), ("dp", 2), ("region", 4), ("dp", 4)]
    width = sizes["dp"]
    steps = []
    for flip0, flip1 in zip(core + first, core + second):
        perm, bits = [], []
        for device in range(sizes["region"] * width):
            at = {"region": device // width, "dp": device % width}
            axis, bit = flip1 if at["region"] & 1 else flip0
            bits.append(1 if at[axis] & bit else 0)
            at[axis] ^= bit
            perm.append((device, at["region"] * width + at["dp"]))
        steps.append((perm, bits))
    return steps


def all_sum(buffers, sizes):
    axes = ("region", "dp")
    me = lax.axis_index("region") * sizes["dp"] + lax.axis_index("dp")
    steps = halving_plan(sizes)
    for perm, bits in steps:
        upper = jnp.asarray(bits, jnp.int32)[me] == 1
        keeps, sends = [], []
        for value in buffers:
            half = value.shape[0] // 2
            low, high = value[:half], value[half:]
            keeps.append(jnp.where(upper, high, low))
            sends.append(jnp.where(upper, low, high))
        got = lax.ppermute(tuple(sends), axes, perm)
        buffers = tuple(k + g for k, g in zip(keeps, got))
    for perm, bits in reversed(steps):
        upper = jnp.asarray(bits, jnp.int32)[me] == 1
        got = lax.ppermute(buffers, axes, perm)
        buffers = tuple(
            jnp.concatenate([jnp.where(upper, g, v), jnp.where(upper, v, g)], axis=0)
            for v, g in zip(buffers, got)
        )
    return buffers


def local(cells, cell_weight, cell_cluster, cluster_edges, labels, w_self, w_nbr, w_out):
    region = lax.axis_index("region")
    owned = cluster_edges.shape[1]
    degree = cluster_edges.shape[2]
    weighted = (cell_weight[..., None] * cells.astype(jnp.float32)).astype(jnp.bfloat16)
    relative = cell_cluster - (region - 1) * owned
    numer_three, denom_three = accumulate(relative[0], weighted[0], cell_weight[0], 3 * owned)
    above_numer, above_denom = passed_along(
        (numer_three[:, :owned], denom_three[:, :owned]), "region", -1
    )
    below_numer, below_denom = passed_along(
        (numer_three[:, 2 * owned :], denom_three[:, 2 * owned :]), "region", 1
    )
    numer = numer_three[:, owned : 2 * owned] + above_numer + below_numer
    denom = denom_three[:, owned : 2 * owned] + above_denom + below_denom
    pooled = (numer / denom[..., None]).astype(jnp.bfloat16)
    table = padded(pooled, (("region", 1),), owned)
    targets = cluster_edges - (region - 1) * owned
    width = 3 * owned
    slots = jnp.arange(width, dtype=jnp.int32)
    tally = jnp.zeros((pooled.shape[0], owned, width), jnp.float32)
    for which in range(degree):
        tally = tally + (targets[:, :, which, None] == slots[None, None, :]).astype(jnp.float32)
    agg = (
        jnp.einsum(
            "ekj,ejf->ekf", tally.astype(jnp.bfloat16), table, preferred_element_type=jnp.float32
        )
        / degree
    ).astype(jnp.bfloat16)
    zval = jnp.einsum("ekf,fh->ekh", pooled, w_self, preferred_element_type=jnp.float32)
    zval = zval + jnp.einsum("ekf,fh->ekh", agg, w_nbr, preferred_element_type=jnp.float32)
    sig = jax.nn.sigmoid(zval)
    units = (zval * sig).astype(jnp.bfloat16)
    scores = jnp.einsum("ekh,hc->ekc", units, w_out, preferred_element_type=jnp.float32)
    events = lax.axis_size("dp") * cells.shape[0]
    classes = jnp.arange(w_out.shape[1], dtype=jnp.int32)
    target = (labels[..., None] == classes[None, None, :]).astype(jnp.float32)
    d_logits = ((jax.nn.sigmoid(scores) - target) / events).astype(jnp.bfloat16)
    grad_head = jnp.einsum("ekh,ekc->ch", units, d_logits, preferred_element_type=jnp.float32)
    d_units = jnp.einsum("ekc,hc->ekh", d_logits, w_out, preferred_element_type=jnp.float32)
    d_z = (d_units * sig * (1.0 + zval * (1.0 - sig))).astype(jnp.bfloat16)
    grad_own = jnp.einsum("ekf,ekh->fh", pooled, d_z, preferred_element_type=jnp.float32)
    grad_side = jnp.einsum("ekf,ekh->fh", agg, d_z, preferred_element_type=jnp.float32)
    sizes = {"region": lax.axis_size("region"), "dp": lax.axis_size("dp")}
    hid = grad_own.shape[1]
    grads, head = all_sum(
        (jnp.concatenate([grad_own, grad_side], axis=0), grad_head.reshape(-1)), sizes
    )
    grad_own, grad_side = grads[: pooled.shape[2]], grads[pooled.shape[2] :]
    grad_head = head.reshape(-1, hid).T
    return (scores, grad_own, grad_side, grad_head)


def solution(mesh):
    return jax.shard_map(
        local,
        mesh=mesh,
        in_specs=(
            P("dp", "region", None),
            P("dp", "region"),
            P("dp", "region"),
            P("dp", "region", None),
            P("dp", "region"),
            P(),
            P(),
            P(),
        ),
        out_specs=(P("dp", "region", None), P(), P(), P()),
        check_vma=False,
    )
```

```python
import jax
import jax.numpy as jnp
from jax import lax
from jax.experimental import pallas as pl
from jax.sharding import PartitionSpec as P


def passed_along(value, axis, steps):
    count = lax.axis_size(axis)
    initial, last = (max(0, -steps), min(count, count - steps))
    return lax.ppermute(value, axis, [(source, source + steps) for source in range(initial, last)])


def padded(block, sides, width):
    for axis, dim in sides:
        count = lax.axis_size(axis)
        forward = [(i, i + 1) for i in range(count - 1)]
        backward = [(target, source) for source, target in forward]
        low = lax.ppermute(
            lax.slice_in_dim(block, block.shape[dim] - width, None, axis=dim), axis, forward
        )
        high = lax.ppermute(lax.slice_in_dim(block, 0, width, axis=dim), axis, backward)
        block = jnp.concatenate([low, block, high], axis=dim)
    return block


def pooled_sums_kernel(ids_ref, split_ref, cells_ref, numer_ref, denom_ref):
    @pl.when(pl.program_id(0) == 0)
    def _():
        numer_ref[...] = jnp.zeros_like(numer_ref)
        denom_ref[...] = jnp.zeros_like(denom_ref)

    width = numer_ref.shape[0]
    block = ids_ref.shape[1]
    lanes = denom_ref.shape[1]
    slots = lax.broadcasted_iota(jnp.int32, (width, block), 0)
    member = (ids_ref[...] == slots).astype(jnp.bfloat16)
    split = split_ref[...]
    pad = jnp.zeros((lanes - split.shape[0], block), jnp.float32)
    columns = jnp.concatenate([split, pad], axis=0).T
    lane = lax.broadcasted_iota(jnp.int32, (block, lanes), 1)
    parts = jnp.where(lane < 3, columns, 0.0).astype(jnp.bfloat16)
    weight = columns[:, 3:4]
    weighted = (weight * cells_ref[...].astype(jnp.float32)).astype(jnp.bfloat16)
    numer_ref[...] += jnp.dot(member, weighted, preferred_element_type=jnp.float32)
    denom_ref[...] += jnp.dot(member, parts, preferred_element_type=jnp.float32)


def accumulate(cluster_ids, cells, weights, width):
    length, feats = cells.shape
    high = lax.reduce_precision(weights, exponent_bits=8, mantissa_bits=7)
    rest = weights - high
    middle = lax.reduce_precision(rest, exponent_bits=8, mantissa_bits=7)
    low = rest - middle
    zero = jnp.zeros_like(weights)
    split = jnp.stack([high, middle, low, weights, zero, zero, zero, zero], axis=0)
    block = min(1024, length)
    lanes = 128
    numer, denom = pl.pallas_call(
        pooled_sums_kernel,
        grid=(length // block,),
        in_specs=[
            pl.BlockSpec((1, block), lambda i: (0, i)),
            pl.BlockSpec((8, block), lambda i: (0, i)),
            pl.BlockSpec((block, feats), lambda i: (i, 0)),
        ],
        out_specs=[
            pl.BlockSpec((width, feats), lambda i: (0, 0)),
            pl.BlockSpec((width, lanes), lambda i: (0, 0)),
        ],
        out_shape=[
            jax.ShapeDtypeStruct((width, feats), jnp.float32),
            jax.ShapeDtypeStruct((width, lanes), jnp.float32),
        ],
        cost_estimate=pl.CostEstimate(
            flops=2 * width * length * (feats + lanes),
            bytes_accessed=length * (feats * 2 + 36) + width * (feats + lanes) * 4,
            transcendentals=0,
        ),
    )(cluster_ids.reshape(1, length), split, cells)
    total = denom[:, 0] + denom[:, 1] + denom[:, 2]
    return numer[None], total[None]


def halving_plan(sizes):
    core = [("region", 1)]
    first = [("region", 2), ("dp", 8), ("dp", 1), ("region", 4), ("dp", 16), ("dp", 2), ("dp", 4)]
    second = [("dp", 8), ("dp", 1), ("region", 2), ("dp", 16), ("dp", 2), ("region", 4), ("dp", 4)]
    width = sizes["dp"]
    steps = []
    for flip0, flip1 in zip(core + first, core + second):
        perm, bits = [], []
        for device in range(sizes["region"] * width):
            at = {"region": device // width, "dp": device % width}
            axis, bit = flip1 if at["region"] & 1 else flip0
            bits.append(1 if at[axis] & bit else 0)
            at[axis] ^= bit
            perm.append((device, at["region"] * width + at["dp"]))
        steps.append((perm, bits))
    return steps


def all_sum(buffers, sizes):
    axes = ("region", "dp")
    me = lax.axis_index("region") * sizes["dp"] + lax.axis_index("dp")
    steps = halving_plan(sizes)
    for perm, bits in steps:
        upper = jnp.asarray(bits, jnp.int32)[me] == 1
        keeps, sends = [], []
        for value in buffers:
            half = value.shape[0] // 2
            low, high = value[:half], value[half:]
            keeps.append(jnp.where(upper, high, low))
            sends.append(jnp.where(upper, low, high))
        got = lax.ppermute(tuple(sends), axes, perm)
        buffers = tuple(k + g for k, g in zip(keeps, got))
    for perm, bits in reversed(steps):
        upper = jnp.asarray(bits, jnp.int32)[me] == 1
        got = lax.ppermute(buffers, axes, perm)
        buffers = tuple(
            jnp.concatenate([jnp.where(upper, g, v), jnp.where(upper, v, g)], axis=0)
            for v, g in zip(buffers, got)
        )
    return buffers


def local(cells, cell_weight, cell_cluster, cluster_edges, labels, w_self, w_nbr, w_out):
    region = lax.axis_index("region")
    owned = cluster_edges.shape[1]
    degree = cluster_edges.shape[2]
    relative = cell_cluster - (region - 1) * owned
    numer_three, denom_three = accumulate(relative[0], cells[0], cell_weight[0], 3 * owned)
    above_numer, above_denom = passed_along(
        (numer_three[:, :owned], denom_three[:, :owned]), "region", -1
    )
    below_numer, below_denom = passed_along(
        (numer_three[:, 2 * owned :], denom_three[:, 2 * owned :]), "region", 1
    )
    numer = numer_three[:, owned : 2 * owned] + above_numer + below_numer
    denom = denom_three[:, owned : 2 * owned] + above_denom + below_denom
    pooled = (numer / denom[..., None]).astype(jnp.bfloat16)
    table = padded(pooled, (("region", 1),), owned)
    targets = cluster_edges - (region - 1) * owned
    width = 3 * owned
    slots = jnp.arange(width, dtype=jnp.int32)
    tally = jnp.zeros((pooled.shape[0], owned, width), jnp.float32)
    for which in range(degree):
        tally = tally + (targets[:, :, which, None] == slots[None, None, :]).astype(jnp.float32)
    agg = (
        jnp.einsum(
            "ekj,ejf->ekf", tally.astype(jnp.bfloat16), table, preferred_element_type=jnp.float32
        )
        / degree
    ).astype(jnp.bfloat16)
    zval = jnp.einsum("ekf,fh->ekh", pooled, w_self, preferred_element_type=jnp.float32)
    zval = zval + jnp.einsum("ekf,fh->ekh", agg, w_nbr, preferred_element_type=jnp.float32)
    sig = jax.nn.sigmoid(zval)
    units = (zval * sig).astype(jnp.bfloat16)
    scores = jnp.einsum("ekh,hc->ekc", units, w_out, preferred_element_type=jnp.float32)
    events = lax.axis_size("dp") * cells.shape[0]
    classes = jnp.arange(w_out.shape[1], dtype=jnp.int32)
    target = (labels[..., None] == classes[None, None, :]).astype(jnp.float32)
    d_logits = ((jax.nn.sigmoid(scores) - target) / events).astype(jnp.bfloat16)
    grad_head = jnp.einsum("ekh,ekc->ch", units, d_logits, preferred_element_type=jnp.float32)
    d_units = jnp.einsum("ekc,hc->ekh", d_logits, w_out, preferred_element_type=jnp.float32)
    d_z = (d_units * sig * (1.0 + zval * (1.0 - sig))).astype(jnp.bfloat16)
    grad_own = jnp.einsum("ekf,ekh->fh", pooled, d_z, preferred_element_type=jnp.float32)
    grad_side = jnp.einsum("ekf,ekh->fh", agg, d_z, preferred_element_type=jnp.float32)
    sizes = {"region": lax.axis_size("region"), "dp": lax.axis_size("dp")}
    hid = grad_own.shape[1]
    grads, head = all_sum(
        (jnp.concatenate([grad_own, grad_side], axis=0), grad_head.reshape(-1)), sizes
    )
    grad_own, grad_side = grads[: pooled.shape[2]], grads[pooled.shape[2] :]
    grad_head = head.reshape(-1, hid).T
    return (scores, grad_own, grad_side, grad_head)


def solution(mesh):
    return jax.shard_map(
        local,
        mesh=mesh,
        in_specs=(
            P("dp", "region", None),
            P("dp", "region"),
            P("dp", "region"),
            P("dp", "region", None),
            P("dp", "region"),
            P(),
            P(),
            P(),
        ),
        out_specs=(P("dp", "region", None), P(), P(), P()),
        check_vma=False,
    )
```

```python
import jax
import jax.numpy as jnp
from jax import lax
from jax.experimental import pallas as pl
from jax.sharding import PartitionSpec as P


def passed_along(value, axis, steps):
    count = lax.axis_size(axis)
    initial, last = (max(0, -steps), min(count, count - steps))
    return lax.ppermute(value, axis, [(source, source + steps) for source in range(initial, last)])


def padded(block, sides, width):
    for axis, dim in sides:
        count = lax.axis_size(axis)
        forward = [(i, i + 1) for i in range(count - 1)]
        backward = [(target, source) for source, target in forward]
        low = lax.ppermute(
            lax.slice_in_dim(block, block.shape[dim] - width, None, axis=dim), axis, forward
        )
        high = lax.ppermute(lax.slice_in_dim(block, 0, width, axis=dim), axis, backward)
        block = jnp.concatenate([low, block, high], axis=dim)
    return block


def pooled_sums_kernel(ids_ref, split_ref, cells_ref, numer_ref, denom_ref):
    @pl.when(pl.program_id(0) == 0)
    def _():
        numer_ref[...] = jnp.zeros_like(numer_ref)
        denom_ref[...] = jnp.zeros_like(denom_ref)

    width = numer_ref.shape[0]
    block = ids_ref.shape[1]
    lanes = denom_ref.shape[1]
    slots = lax.broadcasted_iota(jnp.int32, (width, block), 0)
    member = (ids_ref[...] == slots).astype(jnp.bfloat16)
    split = split_ref[...]
    pad = jnp.zeros((lanes - split.shape[0], block), jnp.float32)
    columns = jnp.concatenate([split, pad], axis=0).T
    lane = lax.broadcasted_iota(jnp.int32, (block, lanes), 1)
    parts = jnp.where(lane < 3, columns, 0.0).astype(jnp.bfloat16)
    weight = columns[:, 3:4]
    weighted = (weight * cells_ref[...].astype(jnp.float32)).astype(jnp.bfloat16)
    numer_ref[...] += jnp.dot(member, weighted, preferred_element_type=jnp.float32)
    denom_ref[...] += jnp.dot(member, parts, preferred_element_type=jnp.float32)


def accumulate(cluster_ids, cells, weights, width):
    length, feats = cells.shape
    high = lax.reduce_precision(weights, exponent_bits=8, mantissa_bits=7)
    rest = weights - high
    middle = lax.reduce_precision(rest, exponent_bits=8, mantissa_bits=7)
    low = rest - middle
    zero = jnp.zeros_like(weights)
    split = jnp.stack([high, middle, low, weights, zero, zero, zero, zero], axis=0)
    block = min(1024, length)
    lanes = 128
    numer, denom = pl.pallas_call(
        pooled_sums_kernel,
        grid=(length // block,),
        in_specs=[
            pl.BlockSpec((1, block), lambda i: (0, i)),
            pl.BlockSpec((8, block), lambda i: (0, i)),
            pl.BlockSpec((block, feats), lambda i: (i, 0)),
        ],
        out_specs=[
            pl.BlockSpec((width, feats), lambda i: (0, 0)),
            pl.BlockSpec((width, lanes), lambda i: (0, 0)),
        ],
        out_shape=[
            jax.ShapeDtypeStruct((width, feats), jnp.float32),
            jax.ShapeDtypeStruct((width, lanes), jnp.float32),
        ],
        cost_estimate=pl.CostEstimate(
            flops=2 * width * length * (feats + lanes),
            bytes_accessed=length * (feats * 2 + 36) + width * (feats + lanes) * 4,
            transcendentals=0,
        ),
    )(cluster_ids.reshape(1, length), split, cells)
    total = denom[:, 0] + denom[:, 1] + denom[:, 2]
    return numer[None], total[None]


def halving_plan(sizes):
    core = [("region", 1)]
    first = [("region", 2), ("dp", 8), ("dp", 1), ("region", 4), ("dp", 16), ("dp", 2), ("dp", 4)]
    second = [("dp", 8), ("dp", 1), ("region", 2), ("dp", 16), ("dp", 2), ("region", 4), ("dp", 4)]
    width = sizes["dp"]
    steps = []
    for flip0, flip1 in zip(core + first, core + second):
        perm = []
        for device in range(sizes["region"] * width):
            at = {"region": device // width, "dp": device % width}
            axis, bit = flip1 if at["region"] & 1 else flip0
            at[axis] ^= bit
            perm.append((device, at["region"] * width + at["dp"]))
        steps.append((perm, flip0, flip1))
    return steps


def upper_half(flip0, flip1):
    core = lax.axis_index("region") % 2
    bit0 = (lax.axis_index(flip0[0]) // flip0[1]) % 2
    bit1 = (lax.axis_index(flip1[0]) // flip1[1]) % 2
    return jnp.where(core == 1, bit1, bit0) == 1


def all_sum(value, sizes, halvings):
    axes = ("region", "dp")
    steps = halving_plan(sizes)
    for perm, flip0, flip1 in steps[:halvings]:
        upper = upper_half(flip0, flip1)
        half = value.shape[0] // 2
        low, high = value[:half], value[half:]
        got = lax.ppermute(jnp.where(upper, low, high), axes, perm)
        value = jnp.where(upper, high, low) + got
    for perm, _, _ in steps[halvings:]:
        value = value + lax.ppermute(value, axes, perm)
    for perm, flip0, flip1 in reversed(steps[:halvings]):
        upper = upper_half(flip0, flip1)
        got = lax.ppermute(value, axes, perm)
        value = jnp.concatenate(
            [jnp.where(upper, got, value), jnp.where(upper, value, got)], axis=0
        )
    return value


def local(cells, cell_weight, cell_cluster, cluster_edges, labels, w_self, w_nbr, w_out):
    region = lax.axis_index("region")
    owned = cluster_edges.shape[1]
    degree = cluster_edges.shape[2]
    relative = cell_cluster - (region - 1) * owned
    numer_three, denom_three = accumulate(relative[0], cells[0], cell_weight[0], 3 * owned)
    above_numer, above_denom = passed_along(
        (numer_three[:, :owned], denom_three[:, :owned]), "region", -1
    )
    below_numer, below_denom = passed_along(
        (numer_three[:, 2 * owned :], denom_three[:, 2 * owned :]), "region", 1
    )
    numer = numer_three[:, owned : 2 * owned] + above_numer + below_numer
    denom = denom_three[:, owned : 2 * owned] + above_denom + below_denom
    pooled = (numer / denom[..., None]).astype(jnp.bfloat16)
    table = padded(pooled, (("region", 1),), owned)
    targets = cluster_edges - (region - 1) * owned
    width = 3 * owned
    slots = jnp.arange(width, dtype=jnp.int32)
    tally = jnp.zeros((pooled.shape[0], owned, width), jnp.float32)
    for which in range(degree):
        tally = tally + (targets[:, :, which, None] == slots[None, None, :]).astype(jnp.float32)
    agg = (
        jnp.einsum(
            "ekj,ejf->ekf", tally.astype(jnp.bfloat16), table, preferred_element_type=jnp.float32
        )
        / degree
    ).astype(jnp.bfloat16)
    zval = jnp.einsum("ekf,fh->ekh", pooled, w_self, preferred_element_type=jnp.float32)
    zval = zval + jnp.einsum("ekf,fh->ekh", agg, w_nbr, preferred_element_type=jnp.float32)
    sig = jax.nn.sigmoid(zval)
    units = (zval * sig).astype(jnp.bfloat16)
    scores = jnp.einsum("ekh,hc->ekc", units, w_out, preferred_element_type=jnp.float32)
    events = lax.axis_size("dp") * cells.shape[0]
    classes = jnp.arange(w_out.shape[1], dtype=jnp.int32)
    target = (labels[..., None] == classes[None, None, :]).astype(jnp.float32)
    d_logits = ((jax.nn.sigmoid(scores) - target) / events).astype(jnp.bfloat16)
    grad_head = jnp.einsum("ekh,ekc->hc", units, d_logits, preferred_element_type=jnp.float32)
    d_units = jnp.einsum("ekc,hc->ekh", d_logits, w_out, preferred_element_type=jnp.float32)
    d_z = (d_units * sig * (1.0 + zval * (1.0 - sig))).astype(jnp.bfloat16)
    grad_own = jnp.einsum("ekf,ekh->fh", pooled, d_z, preferred_element_type=jnp.float32)
    grad_side = jnp.einsum("ekf,ekh->fh", agg, d_z, preferred_element_type=jnp.float32)
    sizes = {"region": lax.axis_size("region"), "dp": lax.axis_size("dp")}
    feats, hid = grad_own.shape
    rows = 2 * feats
    packed = jnp.concatenate(
        [jnp.concatenate([grad_own, grad_side], axis=0), grad_head.reshape(rows, -1)], axis=1
    )
    packed = all_sum(packed, sizes, 4)
    grad_own, grad_side = packed[:feats, :hid], packed[feats:, :hid]
    grad_head = packed[:, hid:].reshape(hid, -1)
    return (scores, grad_own, grad_side, grad_head)


def solution(mesh):
    return jax.shard_map(
        local,
        mesh=mesh,
        in_specs=(
            P("dp", "region", None),
            P("dp", "region"),
            P("dp", "region"),
            P("dp", "region", None),
            P("dp", "region"),
            P(),
            P(),
            P(),
        ),
        out_specs=(P("dp", "region", None), P(), P(), P()),
        check_vma=False,
    )
```

```python
import jax
import jax.numpy as jnp
from jax import lax
from jax.experimental import pallas as pl
from jax.sharding import PartitionSpec as P


def passed_along(value, axis, steps):
    count = lax.axis_size(axis)
    initial, last = (max(0, -steps), min(count, count - steps))
    return lax.ppermute(value, axis, [(source, source + steps) for source in range(initial, last)])


def padded(block, sides, width):
    for axis, dim in sides:
        count = lax.axis_size(axis)
        forward = [(i, i + 1) for i in range(count - 1)]
        backward = [(target, source) for source, target in forward]
        low = lax.ppermute(
            lax.slice_in_dim(block, block.shape[dim] - width, None, axis=dim), axis, forward
        )
        high = lax.ppermute(lax.slice_in_dim(block, 0, width, axis=dim), axis, backward)
        block = jnp.concatenate([low, block, high], axis=dim)
    return block


def pooled_sums_kernel(ids_ref, split_ref, cells_ref, numer_ref, denom_ref):
    @pl.when(pl.program_id(0) == 0)
    def _():
        numer_ref[...] = jnp.zeros_like(numer_ref)
        denom_ref[...] = jnp.zeros_like(denom_ref)

    width = numer_ref.shape[0]
    block = ids_ref.shape[1]
    lanes = denom_ref.shape[1]
    slots = lax.broadcasted_iota(jnp.int32, (width, block), 0)
    member = (ids_ref[...] == slots).astype(jnp.bfloat16)
    split = split_ref[...]
    pad = jnp.zeros((lanes - split.shape[0], block), jnp.float32)
    columns = jnp.concatenate([split, pad], axis=0).T
    lane = lax.broadcasted_iota(jnp.int32, (block, lanes), 1)
    parts = jnp.where(lane < 3, columns, 0.0).astype(jnp.bfloat16)
    weight = columns[:, 3:4]
    weighted = (weight * cells_ref[...].astype(jnp.float32)).astype(jnp.bfloat16)
    numer_ref[...] += jnp.dot(member, weighted, preferred_element_type=jnp.float32)
    denom_ref[...] += jnp.dot(member, parts, preferred_element_type=jnp.float32)


def accumulate(cluster_ids, cells, weights, width):
    length, feats = cells.shape
    high = lax.reduce_precision(weights, exponent_bits=8, mantissa_bits=7)
    rest = weights - high
    middle = lax.reduce_precision(rest, exponent_bits=8, mantissa_bits=7)
    low = rest - middle
    zero = jnp.zeros_like(weights)
    split = jnp.stack([high, middle, low, weights, zero, zero, zero, zero], axis=0)
    block = min(1024, length)
    lanes = 128
    numer, denom = pl.pallas_call(
        pooled_sums_kernel,
        grid=(length // block,),
        in_specs=[
            pl.BlockSpec((1, block), lambda i: (0, i)),
            pl.BlockSpec((8, block), lambda i: (0, i)),
            pl.BlockSpec((block, feats), lambda i: (i, 0)),
        ],
        out_specs=[
            pl.BlockSpec((width, feats), lambda i: (0, 0)),
            pl.BlockSpec((width, lanes), lambda i: (0, 0)),
        ],
        out_shape=[
            jax.ShapeDtypeStruct((width, feats), jnp.float32),
            jax.ShapeDtypeStruct((width, lanes), jnp.float32),
        ],
        cost_estimate=pl.CostEstimate(
            flops=2 * width * length * (feats + lanes),
            bytes_accessed=length * (feats * 2 + 36) + width * (feats + lanes) * 4,
            transcendentals=0,
        ),
    )(cluster_ids.reshape(1, length), split, cells)
    total = denom[:, 0] + denom[:, 1] + denom[:, 2]
    return numer[None], total[None]


def halving_plan(sizes):
    core = [("region", 1)]
    first = [("region", 2), ("dp", 8), ("dp", 1), ("region", 4), ("dp", 16), ("dp", 2), ("dp", 4)]
    second = [("dp", 8), ("dp", 1), ("region", 2), ("dp", 16), ("dp", 2), ("region", 4), ("dp", 4)]
    width = sizes["dp"]
    steps = []
    for flip0, flip1 in zip(core + first, core + second):
        perm = []
        for device in range(sizes["region"] * width):
            at = {"region": device // width, "dp": device % width}
            axis, bit = flip1 if at["region"] & 1 else flip0
            at[axis] ^= bit
            perm.append((device, at["region"] * width + at["dp"]))
        steps.append((perm, flip0, flip1))
    return steps


def upper_half(flip0, flip1):
    core = lax.axis_index("region") % 2
    bit0 = (lax.axis_index(flip0[0]) // flip0[1]) % 2
    bit1 = (lax.axis_index(flip1[0]) // flip1[1]) % 2
    return jnp.where(core == 1, bit1, bit0) == 1


def all_sum(value, sizes):
    axes = ("region", "dp")
    steps = halving_plan(sizes)
    for perm, flip0, flip1 in steps:
        upper = upper_half(flip0, flip1)
        half = value.shape[0] // 2
        low, high = value[:half], value[half:]
        got = lax.ppermute(jnp.where(upper, low, high), axes, perm)
        value = jnp.where(upper, high, low) + got
    for index, (perm, flip0, flip1) in enumerate(reversed(steps)):
        upper = upper_half(flip0, flip1)
        got = lax.ppermute(value, axes, perm)
        pair = (jnp.where(upper, got, value), jnp.where(upper, value, got))
        if index == len(steps) - 1:
            return pair
        value = jnp.concatenate(pair, axis=0)


def local(cells, cell_weight, cell_cluster, cluster_edges, labels, w_self, w_nbr, w_out):
    region = lax.axis_index("region")
    owned = cluster_edges.shape[1]
    degree = cluster_edges.shape[2]
    relative = cell_cluster - (region - 1) * owned
    numer_three, denom_three = accumulate(relative[0], cells[0], cell_weight[0], 3 * owned)
    above_numer, above_denom = passed_along(
        (numer_three[:, :owned], denom_three[:, :owned]), "region", -1
    )
    below_numer, below_denom = passed_along(
        (numer_three[:, 2 * owned :], denom_three[:, 2 * owned :]), "region", 1
    )
    numer = numer_three[:, owned : 2 * owned] + above_numer + below_numer
    denom = denom_three[:, owned : 2 * owned] + above_denom + below_denom
    pooled = (numer / denom[..., None]).astype(jnp.bfloat16)
    table = padded(pooled, (("region", 1),), owned)
    targets = cluster_edges - (region - 1) * owned
    width = 3 * owned
    slots = jnp.arange(width, dtype=jnp.int32)
    tally = jnp.zeros((pooled.shape[0], owned, width), jnp.float32)
    for which in range(degree):
        tally = tally + (targets[:, :, which, None] == slots[None, None, :]).astype(jnp.float32)
    agg = (
        jnp.einsum(
            "ekj,ejf->ekf", tally.astype(jnp.bfloat16), table, preferred_element_type=jnp.float32
        )
        / degree
    ).astype(jnp.bfloat16)
    zval = jnp.einsum("ekf,fh->ekh", pooled, w_self, preferred_element_type=jnp.float32)
    zval = zval + jnp.einsum("ekf,fh->ekh", agg, w_nbr, preferred_element_type=jnp.float32)
    sig = jax.nn.sigmoid(zval)
    units = (zval * sig).astype(jnp.bfloat16)
    scores = jnp.einsum("ekh,hc->ekc", units, w_out, preferred_element_type=jnp.float32)
    events = lax.axis_size("dp") * cells.shape[0]
    classes = jnp.arange(w_out.shape[1], dtype=jnp.int32)
    target = (labels[..., None] == classes[None, None, :]).astype(jnp.float32)
    d_logits = ((jax.nn.sigmoid(scores) - target) / events).astype(jnp.bfloat16)
    grad_head = jnp.einsum("ekh,ekc->hc", units, d_logits, preferred_element_type=jnp.float32)
    d_units = jnp.einsum("ekc,hc->ekh", d_logits, w_out, preferred_element_type=jnp.float32)
    d_z = (d_units * sig * (1.0 + zval * (1.0 - sig))).astype(jnp.bfloat16)
    grad_own = jnp.einsum("ekf,ekh->fh", pooled, d_z, preferred_element_type=jnp.float32)
    grad_side = jnp.einsum("ekf,ekh->fh", agg, d_z, preferred_element_type=jnp.float32)
    sizes = {"region": lax.axis_size("region"), "dp": lax.axis_size("dp")}
    feats, hid = grad_own.shape
    rows = 2 * feats
    packed = jnp.concatenate(
        [jnp.concatenate([grad_own, grad_side], axis=0), grad_head.reshape(rows, -1)], axis=1
    )
    first, second = all_sum(packed, sizes)
    grad_own, grad_side = first[:, :hid], second[:, :hid]
    grad_head = jnp.concatenate([first[:, hid:], second[:, hid:]], axis=0).reshape(hid, -1)
    return (scores, grad_own, grad_side, grad_head)


def solution(mesh):
    return jax.shard_map(
        local,
        mesh=mesh,
        in_specs=(
            P("dp", "region", None),
            P("dp", "region"),
            P("dp", "region"),
            P("dp", "region", None),
            P("dp", "region"),
            P(),
            P(),
            P(),
        ),
        out_specs=(P("dp", "region", None), P(), P(), P()),
        check_vma=False,
    )
```

```python
import jax
import jax.numpy as jnp
from jax import lax
from jax.experimental import pallas as pl
from jax.sharding import PartitionSpec as P


def passed_along(value, axis, steps):
    count = lax.axis_size(axis)
    initial, last = (max(0, -steps), min(count, count - steps))
    return lax.ppermute(value, axis, [(source, source + steps) for source in range(initial, last)])


def padded(block, sides, width):
    for axis, dim in sides:
        count = lax.axis_size(axis)
        forward = [(i, i + 1) for i in range(count - 1)]
        backward = [(target, source) for source, target in forward]
        low = lax.ppermute(
            lax.slice_in_dim(block, block.shape[dim] - width, None, axis=dim), axis, forward
        )
        high = lax.ppermute(lax.slice_in_dim(block, 0, width, axis=dim), axis, backward)
        block = jnp.concatenate([low, block, high], axis=dim)
    return block


def pooled_sums_kernel(ids_ref, split_ref, cells_ref, numer_ref, denom_ref):
    @pl.when(pl.program_id(0) == 0)
    def _():
        numer_ref[...] = jnp.zeros_like(numer_ref)
        denom_ref[...] = jnp.zeros_like(denom_ref)

    width = numer_ref.shape[0]
    block = ids_ref.shape[1]
    lanes = denom_ref.shape[1]
    slots = lax.broadcasted_iota(jnp.int32, (width, block), 0)
    member = (ids_ref[...] == slots).astype(jnp.bfloat16)
    split = split_ref[...]
    pad = jnp.zeros((lanes - split.shape[0], block), jnp.float32)
    columns = jnp.concatenate([split, pad], axis=0).T
    lane = lax.broadcasted_iota(jnp.int32, (block, lanes), 1)
    parts = jnp.where(lane < 3, columns, 0.0).astype(jnp.bfloat16)
    weight = columns[:, 3:4]
    weighted = (weight * cells_ref[...].astype(jnp.float32)).astype(jnp.bfloat16)
    numer_ref[...] += jnp.dot(member, weighted, preferred_element_type=jnp.float32)
    denom_ref[...] += jnp.dot(member, parts, preferred_element_type=jnp.float32)


def accumulate(cluster_ids, cells, weights, width):
    length, feats = cells.shape
    high = lax.reduce_precision(weights, exponent_bits=8, mantissa_bits=7)
    rest = weights - high
    middle = lax.reduce_precision(rest, exponent_bits=8, mantissa_bits=7)
    low = rest - middle
    zero = jnp.zeros_like(weights)
    split = jnp.stack([high, middle, low, weights, zero, zero, zero, zero], axis=0)
    block = min(1024, length)
    lanes = 128
    numer, denom = pl.pallas_call(
        pooled_sums_kernel,
        grid=(length // block,),
        in_specs=[
            pl.BlockSpec((1, block), lambda i: (0, i)),
            pl.BlockSpec((8, block), lambda i: (0, i)),
            pl.BlockSpec((block, feats), lambda i: (i, 0)),
        ],
        out_specs=[
            pl.BlockSpec((width, feats), lambda i: (0, 0)),
            pl.BlockSpec((width, lanes), lambda i: (0, 0)),
        ],
        out_shape=[
            jax.ShapeDtypeStruct((width, feats), jnp.float32),
            jax.ShapeDtypeStruct((width, lanes), jnp.float32),
        ],
        cost_estimate=pl.CostEstimate(
            flops=2 * width * length * (feats + lanes),
            bytes_accessed=length * (feats * 2 + 36) + width * (feats + lanes) * 4,
            transcendentals=0,
        ),
    )(cluster_ids.reshape(1, length), split, cells)
    total = denom[:, 0] + denom[:, 1] + denom[:, 2]
    return numer[None], total[None]


def halving_plan(sizes):
    width = sizes["dp"]
    steps = []
    bit = 1
    while bit < sizes["region"]:
        perm = []
        for device in range(sizes["region"] * width):
            region, dp = divmod(device, width)
            perm.append((device, (region ^ bit) * width + dp))
        steps.append((perm, bit))
        bit *= 2
    return steps


def all_sum(value, sizes):
    axes = ("region", "dp")
    steps = halving_plan(sizes)
    for perm, bit in steps:
        upper = (lax.axis_index("region") // bit) % 2 == 1
        half = value.shape[0] // 2
        low, high = value[:half], value[half:]
        got = lax.ppermute(jnp.where(upper, low, high), axes, perm)
        value = jnp.where(upper, high, low) + got
    count = sizes["dp"]
    pieces = value.reshape((count, value.shape[0] // count) + value.shape[1:])
    value = lax.all_to_all(pieces, "dp", 0, 0, tiled=False).sum(axis=0)
    copies = jnp.broadcast_to(value[None], (count,) + value.shape)
    value = lax.all_to_all(copies, "dp", 0, 0, tiled=False)
    value = value.reshape((count * value.shape[1],) + value.shape[2:])
    for index, (perm, bit) in enumerate(reversed(steps)):
        upper = (lax.axis_index("region") // bit) % 2 == 1
        got = lax.ppermute(value, axes, perm)
        pair = (jnp.where(upper, got, value), jnp.where(upper, value, got))
        if index == len(steps) - 1:
            return pair
        value = jnp.concatenate(pair, axis=0)


def local(cells, cell_weight, cell_cluster, cluster_edges, labels, w_self, w_nbr, w_out):
    region = lax.axis_index("region")
    owned = cluster_edges.shape[1]
    degree = cluster_edges.shape[2]
    relative = cell_cluster - (region - 1) * owned
    numer_three, denom_three = accumulate(relative[0], cells[0], cell_weight[0], 3 * owned)
    above_numer, above_denom = passed_along(
        (numer_three[:, :owned], denom_three[:, :owned]), "region", -1
    )
    below_numer, below_denom = passed_along(
        (numer_three[:, 2 * owned :], denom_three[:, 2 * owned :]), "region", 1
    )
    numer = numer_three[:, owned : 2 * owned] + above_numer + below_numer
    denom = denom_three[:, owned : 2 * owned] + above_denom + below_denom
    pooled = (numer / denom[..., None]).astype(jnp.bfloat16)
    table = padded(pooled, (("region", 1),), owned)
    targets = cluster_edges - (region - 1) * owned
    width = 3 * owned
    slots = jnp.arange(width, dtype=jnp.int32)
    tally = jnp.zeros((pooled.shape[0], owned, width), jnp.float32)
    for which in range(degree):
        tally = tally + (targets[:, :, which, None] == slots[None, None, :]).astype(jnp.float32)
    agg = (
        jnp.einsum(
            "ekj,ejf->ekf", tally.astype(jnp.bfloat16), table, preferred_element_type=jnp.float32
        )
        / degree
    ).astype(jnp.bfloat16)
    zval = jnp.einsum("ekf,fh->ekh", pooled, w_self, preferred_element_type=jnp.float32)
    zval = zval + jnp.einsum("ekf,fh->ekh", agg, w_nbr, preferred_element_type=jnp.float32)
    sig = jax.nn.sigmoid(zval)
    units = (zval * sig).astype(jnp.bfloat16)
    scores = jnp.einsum("ekh,hc->ekc", units, w_out, preferred_element_type=jnp.float32)
    events = lax.axis_size("dp") * cells.shape[0]
    classes = jnp.arange(w_out.shape[1], dtype=jnp.int32)
    target = (labels[..., None] == classes[None, None, :]).astype(jnp.float32)
    d_logits = ((jax.nn.sigmoid(scores) - target) / events).astype(jnp.bfloat16)
    grad_head = jnp.einsum("ekh,ekc->hc", units, d_logits, preferred_element_type=jnp.float32)
    d_units = jnp.einsum("ekc,hc->ekh", d_logits, w_out, preferred_element_type=jnp.float32)
    d_z = (d_units * sig * (1.0 + zval * (1.0 - sig))).astype(jnp.bfloat16)
    grad_own = jnp.einsum("ekf,ekh->fh", pooled, d_z, preferred_element_type=jnp.float32)
    grad_side = jnp.einsum("ekf,ekh->fh", agg, d_z, preferred_element_type=jnp.float32)
    sizes = {"region": lax.axis_size("region"), "dp": lax.axis_size("dp")}
    feats, hid = grad_own.shape
    rows = 2 * feats
    packed = jnp.concatenate(
        [jnp.concatenate([grad_own, grad_side], axis=0), grad_head.reshape(rows, -1)], axis=1
    )
    first, second = all_sum(packed, sizes)
    grad_own, grad_side = first[:, :hid], second[:, :hid]
    grad_head = jnp.concatenate([first[:, hid:], second[:, hid:]], axis=0).reshape(hid, -1)
    return (scores, grad_own, grad_side, grad_head)


def solution(mesh):
    return jax.shard_map(
        local,
        mesh=mesh,
        in_specs=(
            P("dp", "region", None),
            P("dp", "region"),
            P("dp", "region"),
            P("dp", "region", None),
            P("dp", "region"),
            P(),
            P(),
            P(),
        ),
        out_specs=(P("dp", "region", None), P(), P(), P()),
        check_vma=False,
    )
```

```python
import jax
import jax.numpy as jnp
from jax import lax
from jax.experimental import pallas as pl
from jax.sharding import PartitionSpec as P


def passed_along(value, axis, steps):
    count = lax.axis_size(axis)
    initial, last = (max(0, -steps), min(count, count - steps))
    return lax.ppermute(value, axis, [(source, source + steps) for source in range(initial, last)])


def padded(block, sides, width):
    for axis, dim in sides:
        count = lax.axis_size(axis)
        forward = [(i, i + 1) for i in range(count - 1)]
        backward = [(target, source) for source, target in forward]
        low = lax.ppermute(
            lax.slice_in_dim(block, block.shape[dim] - width, None, axis=dim), axis, forward
        )
        high = lax.ppermute(lax.slice_in_dim(block, 0, width, axis=dim), axis, backward)
        block = jnp.concatenate([low, block, high], axis=dim)
    return block


def pooled_sums_kernel(ids_ref, split_ref, cells_ref, sums_ref):
    @pl.when(pl.program_id(0) == 0)
    def _():
        sums_ref[...] = jnp.zeros_like(sums_ref)

    width = sums_ref.shape[0]
    block = ids_ref.shape[1]
    feats = cells_ref.shape[1]
    lanes = sums_ref.shape[1] - feats
    slots = lax.broadcasted_iota(jnp.int32, (width, block), 0)
    member = (ids_ref[...] == slots).astype(jnp.bfloat16)
    split = split_ref[...]
    pad = jnp.zeros((lanes - split.shape[0], block), jnp.float32)
    columns = jnp.concatenate([split, pad], axis=0).T
    lane = lax.broadcasted_iota(jnp.int32, (block, lanes), 1)
    parts = jnp.where(lane < 3, columns, 0.0).astype(jnp.bfloat16)
    weight = columns[:, 3:4]
    weighted = (weight * cells_ref[...].astype(jnp.float32)).astype(jnp.bfloat16)
    sums_ref[:, :feats] += jnp.dot(member, weighted, preferred_element_type=jnp.float32)
    sums_ref[:, feats:] += jnp.dot(member, parts, preferred_element_type=jnp.float32)


def accumulate(cluster_ids, cells, weights, width):
    length, feats = cells.shape
    high = lax.reduce_precision(weights, exponent_bits=8, mantissa_bits=7)
    rest = weights - high
    middle = lax.reduce_precision(rest, exponent_bits=8, mantissa_bits=7)
    low = rest - middle
    zero = jnp.zeros_like(weights)
    split = jnp.stack([high, middle, low, weights, zero, zero, zero, zero], axis=0)
    block = min(1024, length)
    lanes = 128
    sums = pl.pallas_call(
        pooled_sums_kernel,
        grid=(length // block,),
        in_specs=[
            pl.BlockSpec((1, block), lambda i: (0, i)),
            pl.BlockSpec((8, block), lambda i: (0, i)),
            pl.BlockSpec((block, feats), lambda i: (i, 0)),
        ],
        out_specs=pl.BlockSpec((width, feats + lanes), lambda i: (0, 0)),
        out_shape=jax.ShapeDtypeStruct((width, feats + lanes), jnp.float32),
        cost_estimate=pl.CostEstimate(
            flops=2 * width * length * (feats + lanes),
            bytes_accessed=length * (feats * 2 + 36) + width * (feats + lanes) * 4,
            transcendentals=0,
        ),
    )(cluster_ids.reshape(1, length), split, cells)
    return sums


def halving_plan(sizes):
    core = [("region", 1)]
    first = [("region", 2), ("dp", 8), ("dp", 1), ("region", 4), ("dp", 16), ("dp", 2), ("dp", 4)]
    second = [("dp", 8), ("dp", 1), ("region", 2), ("dp", 16), ("dp", 2), ("region", 4), ("dp", 4)]
    width = sizes["dp"]
    steps = []
    for flip0, flip1 in zip(core + first, core + second):
        perm = []
        for device in range(sizes["region"] * width):
            at = {"region": device // width, "dp": device % width}
            axis, bit = flip1 if at["region"] & 1 else flip0
            at[axis] ^= bit
            perm.append((device, at["region"] * width + at["dp"]))
        steps.append((perm, flip0, flip1))
    return steps


def upper_half(flip0, flip1):
    core = lax.axis_index("region") % 2
    bit0 = (lax.axis_index(flip0[0]) // flip0[1]) % 2
    bit1 = (lax.axis_index(flip1[0]) // flip1[1]) % 2
    return jnp.where(core == 1, bit1, bit0) == 1


def all_sum(value, sizes, halvings):
    axes = ("region", "dp")
    steps = halving_plan(sizes)
    for perm, flip0, flip1 in steps[:halvings]:
        upper = upper_half(flip0, flip1)
        half = value.shape[0] // 2
        low, high = value[:half], value[half:]
        got = lax.ppermute(jnp.where(upper, low, high), axes, perm)
        value = jnp.where(upper, high, low) + got
    for perm, _, _ in steps[halvings:]:
        value = value + lax.ppermute(value, axes, perm)
    for perm, flip0, flip1 in reversed(steps[:halvings]):
        upper = upper_half(flip0, flip1)
        got = lax.ppermute(value, axes, perm)
        value = jnp.concatenate(
            [jnp.where(upper, got, value), jnp.where(upper, value, got)], axis=0
        )
    return value


def local(cells, cell_weight, cell_cluster, cluster_edges, labels, w_self, w_nbr, w_out):
    region = lax.axis_index("region")
    owned = cluster_edges.shape[1]
    degree = cluster_edges.shape[2]
    relative = cell_cluster - (region - 1) * owned
    sums = accumulate(relative[0], cells[0], cell_weight[0], 3 * owned)
    above = passed_along(sums[:owned], "region", -1)
    below = passed_along(sums[2 * owned :], "region", 1)
    total = (sums[owned : 2 * owned] + above + below)[None]
    feats = cells.shape[2]
    numer = total[..., :feats]
    denom = total[..., feats] + total[..., feats + 1] + total[..., feats + 2]
    pooled = (numer / denom[..., None]).astype(jnp.bfloat16)
    table = padded(pooled, (("region", 1),), owned)
    targets = cluster_edges - (region - 1) * owned
    width = 3 * owned
    slots = jnp.arange(width, dtype=jnp.int32)
    tally = jnp.zeros((pooled.shape[0], owned, width), jnp.float32)
    for which in range(degree):
        tally = tally + (targets[:, :, which, None] == slots[None, None, :]).astype(jnp.float32)
    agg = (
        jnp.einsum(
            "ekj,ejf->ekf", tally.astype(jnp.bfloat16), table, preferred_element_type=jnp.float32
        )
        / degree
    ).astype(jnp.bfloat16)
    zval = jnp.einsum("ekf,fh->ekh", pooled, w_self, preferred_element_type=jnp.float32)
    zval = zval + jnp.einsum("ekf,fh->ekh", agg, w_nbr, preferred_element_type=jnp.float32)
    sig = jax.nn.sigmoid(zval)
    units = (zval * sig).astype(jnp.bfloat16)
    scores = jnp.einsum("ekh,hc->ekc", units, w_out, preferred_element_type=jnp.float32)
    events = lax.axis_size("dp") * cells.shape[0]
    classes = jnp.arange(w_out.shape[1], dtype=jnp.int32)
    target = (labels[..., None] == classes[None, None, :]).astype(jnp.float32)
    d_logits = ((jax.nn.sigmoid(scores) - target) / events).astype(jnp.bfloat16)
    grad_head = jnp.einsum("ekh,ekc->hc", units, d_logits, preferred_element_type=jnp.float32)
    d_units = jnp.einsum("ekc,hc->ekh", d_logits, w_out, preferred_element_type=jnp.float32)
    d_z = (d_units * sig * (1.0 + zval * (1.0 - sig))).astype(jnp.bfloat16)
    grad_own = jnp.einsum("ekf,ekh->fh", pooled, d_z, preferred_element_type=jnp.float32)
    grad_side = jnp.einsum("ekf,ekh->fh", agg, d_z, preferred_element_type=jnp.float32)
    sizes = {"region": lax.axis_size("region"), "dp": lax.axis_size("dp")}
    feats, hid = grad_own.shape
    rows = 2 * feats
    packed = jnp.concatenate(
        [jnp.concatenate([grad_own, grad_side], axis=0), grad_head.reshape(rows, -1)], axis=1
    )
    packed = all_sum(packed, sizes, 4)
    grad_own, grad_side = packed[:feats, :hid], packed[feats:, :hid]
    grad_head = packed[:, hid:].reshape(hid, -1)
    return (scores, grad_own, grad_side, grad_head)


def solution(mesh):
    return jax.shard_map(
        local,
        mesh=mesh,
        in_specs=(
            P("dp", "region", None),
            P("dp", "region"),
            P("dp", "region"),
            P("dp", "region", None),
            P("dp", "region"),
            P(),
            P(),
            P(),
        ),
        out_specs=(P("dp", "region", None), P(), P(), P()),
        check_vma=False,
    )
```

```python
import jax
import jax.numpy as jnp
from jax import lax
from jax.experimental import pallas as pl
from jax.sharding import PartitionSpec as P


def passed_along(value, axis, steps):
    count = lax.axis_size(axis)
    initial, last = (max(0, -steps), min(count, count - steps))
    return lax.ppermute(value, axis, [(source, source + steps) for source in range(initial, last)])


def padded(block, sides, width):
    for axis, dim in sides:
        count = lax.axis_size(axis)
        forward = [(i, i + 1) for i in range(count - 1)]
        backward = [(target, source) for source, target in forward]
        low = lax.ppermute(
            lax.slice_in_dim(block, block.shape[dim] - width, None, axis=dim), axis, forward
        )
        high = lax.ppermute(lax.slice_in_dim(block, 0, width, axis=dim), axis, backward)
        block = jnp.concatenate([low, block, high], axis=dim)
    return block


def pooled_sums_kernel(ids_ref, split_ref, cells_ref, sums_ref):
    @pl.when(pl.program_id(0) == 0)
    def _():
        sums_ref[...] = jnp.zeros_like(sums_ref)

    width = sums_ref.shape[0]
    block = ids_ref.shape[1]
    feats = cells_ref.shape[1]
    lanes = sums_ref.shape[1] - feats
    slots = lax.broadcasted_iota(jnp.int32, (width, block), 0)
    member = (ids_ref[...] == slots).astype(jnp.bfloat16)
    split = split_ref[...]
    pad = jnp.zeros((lanes - split.shape[0], block), jnp.float32)
    columns = jnp.concatenate([split, pad], axis=0).T
    lane = lax.broadcasted_iota(jnp.int32, (block, lanes), 1)
    parts = jnp.where(lane < 3, columns, 0.0).astype(jnp.bfloat16)
    weight = columns[:, 3:4]
    weighted = (weight * cells_ref[...].astype(jnp.float32)).astype(jnp.bfloat16)
    sums_ref[:, :feats] += jnp.dot(member, weighted, preferred_element_type=jnp.float32)
    sums_ref[:, feats:] += jnp.dot(member, parts, preferred_element_type=jnp.float32)


def accumulate(cluster_ids, cells, weights, width):
    length, feats = cells.shape
    high = lax.reduce_precision(weights, exponent_bits=8, mantissa_bits=7)
    rest = weights - high
    middle = lax.reduce_precision(rest, exponent_bits=8, mantissa_bits=7)
    low = rest - middle
    zero = jnp.zeros_like(weights)
    split = jnp.stack([high, middle, low, weights, zero, zero, zero, zero], axis=0)
    block = min(2048, length)
    lanes = 128
    sums = pl.pallas_call(
        pooled_sums_kernel,
        grid=(length // block,),
        in_specs=[
            pl.BlockSpec((1, block), lambda i: (0, i)),
            pl.BlockSpec((8, block), lambda i: (0, i)),
            pl.BlockSpec((block, feats), lambda i: (i, 0)),
        ],
        out_specs=pl.BlockSpec((width, feats + lanes), lambda i: (0, 0)),
        out_shape=jax.ShapeDtypeStruct((width, feats + lanes), jnp.float32),
        cost_estimate=pl.CostEstimate(
            flops=2 * width * length * (feats + lanes),
            bytes_accessed=length * (feats * 2 + 36) + width * (feats + lanes) * 4,
            transcendentals=0,
        ),
    )(cluster_ids.reshape(1, length), split, cells)
    return sums


def halving_plan(sizes):
    core = [("region", 1)]
    first = [("region", 2), ("dp", 8), ("dp", 1), ("region", 4), ("dp", 16), ("dp", 2), ("dp", 4)]
    second = [("dp", 8), ("dp", 1), ("region", 2), ("dp", 16), ("dp", 2), ("region", 4), ("dp", 4)]
    width = sizes["dp"]
    steps = []
    for flip0, flip1 in zip(core + first, core + second):
        perm = []
        for device in range(sizes["region"] * width):
            at = {"region": device // width, "dp": device % width}
            axis, bit = flip1 if at["region"] & 1 else flip0
            at[axis] ^= bit
            perm.append((device, at["region"] * width + at["dp"]))
        steps.append((perm, flip0, flip1))
    return steps


def upper_half(flip0, flip1):
    core = lax.axis_index("region") % 2
    bit0 = (lax.axis_index(flip0[0]) // flip0[1]) % 2
    bit1 = (lax.axis_index(flip1[0]) // flip1[1]) % 2
    return jnp.where(core == 1, bit1, bit0) == 1


def all_sum(value, sizes, halvings):
    axes = ("region", "dp")
    steps = halving_plan(sizes)
    for perm, flip0, flip1 in steps[:halvings]:
        upper = upper_half(flip0, flip1)
        half = value.shape[0] // 2
        low, high = value[:half], value[half:]
        got = lax.ppermute(jnp.where(upper, low, high), axes, perm)
        value = jnp.where(upper, high, low) + got
    for perm, _, _ in steps[halvings:]:
        value = value + lax.ppermute(value, axes, perm)
    value = value.astype(jnp.bfloat16)
    for perm, flip0, flip1 in reversed(steps[:halvings]):
        upper = upper_half(flip0, flip1)
        got = lax.ppermute(value, axes, perm)
        value = jnp.concatenate(
            [jnp.where(upper, got, value), jnp.where(upper, value, got)], axis=0
        )
    return value


def local(cells, cell_weight, cell_cluster, cluster_edges, labels, w_self, w_nbr, w_out):
    region = lax.axis_index("region")
    owned = cluster_edges.shape[1]
    degree = cluster_edges.shape[2]
    relative = cell_cluster - (region - 1) * owned
    sums = accumulate(relative[0], cells[0], cell_weight[0], 3 * owned)
    above = passed_along(sums[:owned], "region", -1)
    below = passed_along(sums[2 * owned :], "region", 1)
    total = (sums[owned : 2 * owned] + above + below)[None]
    feats = cells.shape[2]
    numer = total[..., :feats]
    denom = total[..., feats] + total[..., feats + 1] + total[..., feats + 2]
    pooled = (numer / denom[..., None]).astype(jnp.bfloat16)
    table = padded(pooled, (("region", 1),), owned)
    targets = cluster_edges - (region - 1) * owned
    width = 3 * owned
    slots = jnp.arange(width, dtype=jnp.int32)
    tally = jnp.zeros((pooled.shape[0], owned, width), jnp.float32)
    for which in range(degree):
        tally = tally + (targets[:, :, which, None] == slots[None, None, :]).astype(jnp.float32)
    agg = (
        jnp.einsum(
            "ekj,ejf->ekf", tally.astype(jnp.bfloat16), table, preferred_element_type=jnp.float32
        )
        / degree
    ).astype(jnp.bfloat16)
    zval = jnp.einsum("ekf,fh->ekh", pooled, w_self, preferred_element_type=jnp.float32)
    zval = zval + jnp.einsum("ekf,fh->ekh", agg, w_nbr, preferred_element_type=jnp.float32)
    sig = jax.nn.sigmoid(zval)
    units = (zval * sig).astype(jnp.bfloat16)
    scores = jnp.einsum("ekh,hc->ekc", units, w_out, preferred_element_type=jnp.float32)
    events = lax.axis_size("dp") * cells.shape[0]
    classes = jnp.arange(w_out.shape[1], dtype=jnp.int32)
    target = (labels[..., None] == classes[None, None, :]).astype(jnp.float32)
    d_logits = ((jax.nn.sigmoid(scores) - target) / events).astype(jnp.bfloat16)
    grad_head = jnp.einsum("ekh,ekc->hc", units, d_logits, preferred_element_type=jnp.float32)
    d_units = jnp.einsum("ekc,hc->ekh", d_logits, w_out, preferred_element_type=jnp.float32)
    d_z = (d_units * sig * (1.0 + zval * (1.0 - sig))).astype(jnp.bfloat16)
    grad_own = jnp.einsum("ekf,ekh->fh", pooled, d_z, preferred_element_type=jnp.float32)
    grad_side = jnp.einsum("ekf,ekh->fh", agg, d_z, preferred_element_type=jnp.float32)
    sizes = {"region": lax.axis_size("region"), "dp": lax.axis_size("dp")}
    feats, hid = grad_own.shape
    rows = 2 * feats
    packed = jnp.concatenate(
        [jnp.concatenate([grad_own, grad_side], axis=0), grad_head.reshape(rows, -1)], axis=1
    )
    packed = all_sum(packed, sizes, 4)
    packed = packed.astype(jnp.float32)
    grad_own, grad_side = packed[:feats, :hid], packed[feats:, :hid]
    grad_head = packed[:, hid:].reshape(hid, -1)
    return (scores, grad_own, grad_side, grad_head)


def solution(mesh):
    return jax.shard_map(
        local,
        mesh=mesh,
        in_specs=(
            P("dp", "region", None),
            P("dp", "region"),
            P("dp", "region"),
            P("dp", "region", None),
            P("dp", "region"),
            P(),
            P(),
            P(),
        ),
        out_specs=(P("dp", "region", None), P(), P(), P()),
        check_vma=False,
    )
```

```python
import jax
import jax.numpy as jnp
from jax import lax
from jax.experimental import pallas as pl
from jax.sharding import PartitionSpec as P


def passed_along(value, axis, steps):
    count = lax.axis_size(axis)
    initial, last = (max(0, -steps), min(count, count - steps))
    return lax.ppermute(value, axis, [(source, source + steps) for source in range(initial, last)])


def padded(block, sides, width):
    for axis, dim in sides:
        count = lax.axis_size(axis)
        forward = [(i, i + 1) for i in range(count - 1)]
        backward = [(target, source) for source, target in forward]
        low = lax.ppermute(
            lax.slice_in_dim(block, block.shape[dim] - width, None, axis=dim), axis, forward
        )
        high = lax.ppermute(lax.slice_in_dim(block, 0, width, axis=dim), axis, backward)
        block = jnp.concatenate([low, block, high], axis=dim)
    return block


def pooled_sums_kernel(ids_ref, split_ref, cells_ref, sums_ref):
    @pl.when(pl.program_id(0) == 0)
    def _():
        sums_ref[...] = jnp.zeros_like(sums_ref)

    width = sums_ref.shape[0]
    block = ids_ref.shape[1]
    feats = cells_ref.shape[1]
    lanes = sums_ref.shape[1] - feats
    slots = lax.broadcasted_iota(jnp.int32, (width, block), 0)
    member = (ids_ref[...] == slots).astype(jnp.bfloat16)
    split = split_ref[...]
    pad = jnp.zeros((lanes - split.shape[0], block), jnp.float32)
    columns = jnp.concatenate([split, pad], axis=0).T
    lane = lax.broadcasted_iota(jnp.int32, (block, lanes), 1)
    parts = jnp.where(lane < 3, columns, 0.0).astype(jnp.bfloat16)
    weight = columns[:, 3:4]
    weighted = (weight * cells_ref[...].astype(jnp.float32)).astype(jnp.bfloat16)
    sums_ref[:, :feats] += jnp.dot(member, weighted, preferred_element_type=jnp.float32)
    sums_ref[:, feats:] += jnp.dot(member, parts, preferred_element_type=jnp.float32)


def accumulate(cluster_ids, cells, weights, width):
    length, feats = cells.shape
    high = lax.reduce_precision(weights, exponent_bits=8, mantissa_bits=7)
    rest = weights - high
    middle = lax.reduce_precision(rest, exponent_bits=8, mantissa_bits=7)
    low = rest - middle
    zero = jnp.zeros_like(weights)
    split = jnp.stack([high, middle, low, weights, zero, zero, zero, zero], axis=0)
    block = min(2048, length)
    lanes = 128
    sums = pl.pallas_call(
        pooled_sums_kernel,
        grid=(length // block,),
        in_specs=[
            pl.BlockSpec((1, block), lambda i: (0, i)),
            pl.BlockSpec((8, block), lambda i: (0, i)),
            pl.BlockSpec((block, feats), lambda i: (i, 0)),
        ],
        out_specs=pl.BlockSpec((width, feats + lanes), lambda i: (0, 0)),
        out_shape=jax.ShapeDtypeStruct((width, feats + lanes), jnp.float32),
        cost_estimate=pl.CostEstimate(
            flops=2 * width * length * (feats + lanes),
            bytes_accessed=length * (feats * 2 + 36) + width * (feats + lanes) * 4,
            transcendentals=0,
        ),
    )(cluster_ids.reshape(1, length), split, cells)
    return sums


def halving_plan(sizes):
    core = [("region", 1)]
    first = [("region", 2), ("dp", 8), ("dp", 1), ("region", 4), ("dp", 16), ("dp", 2), ("dp", 4)]
    second = [("dp", 8), ("dp", 1), ("region", 2), ("dp", 16), ("dp", 2), ("region", 4), ("dp", 4)]
    width = sizes["dp"]
    steps = []
    for flip0, flip1 in zip(core + first, core + second):
        perm = []
        for device in range(sizes["region"] * width):
            at = {"region": device // width, "dp": device % width}
            axis, bit = flip1 if at["region"] & 1 else flip0
            at[axis] ^= bit
            perm.append((device, at["region"] * width + at["dp"]))
        steps.append((perm, flip0, flip1))
    return steps


def upper_half(flip0, flip1):
    core = lax.axis_index("region") % 2
    bit0 = (lax.axis_index(flip0[0]) // flip0[1]) % 2
    bit1 = (lax.axis_index(flip1[0]) // flip1[1]) % 2
    return jnp.where(core == 1, bit1, bit0) == 1


def all_sum(value, sizes, halvings):
    axes = ("region", "dp")
    steps = halving_plan(sizes)
    for perm, flip0, flip1 in steps[:halvings]:
        upper = upper_half(flip0, flip1)
        half = value.shape[0] // 2
        low, high = value[:half], value[half:]
        got = lax.ppermute(jnp.where(upper, low, high), axes, perm)
        value = jnp.where(upper, high, low) + got
    for perm, _, _ in steps[halvings:]:
        value = value + lax.ppermute(value, axes, perm)
    value = value.astype(jnp.bfloat16)
    for perm, flip0, flip1 in reversed(steps[:halvings]):
        upper = upper_half(flip0, flip1)
        got = lax.ppermute(value, axes, perm)
        value = jnp.concatenate(
            [jnp.where(upper, got, value), jnp.where(upper, value, got)], axis=0
        )
    return value


def local(cells, cell_weight, cell_cluster, cluster_edges, labels, w_self, w_nbr, w_out):
    region = lax.axis_index("region")
    owned = cluster_edges.shape[1]
    degree = cluster_edges.shape[2]
    relative = cell_cluster - (region - 1) * owned
    sums = accumulate(relative[0], cells[0], cell_weight[0], 3 * owned)
    above = passed_along(sums[:owned], "region", -1)
    below = passed_along(sums[2 * owned :], "region", 1)
    total = (sums[owned : 2 * owned] + above + below)[None]
    feats = cells.shape[2]
    numer = total[..., :feats]
    denom = total[..., feats] + total[..., feats + 1] + total[..., feats + 2]
    pooled = (numer / denom[..., None]).astype(jnp.bfloat16)
    table = padded(pooled, (("region", 1),), owned)
    targets = cluster_edges - (region - 1) * owned
    width = 3 * owned
    slots = jnp.arange(width, dtype=jnp.int32)
    tally = jnp.zeros((pooled.shape[0], owned, width), jnp.float32)
    for which in range(degree):
        tally = tally + (targets[:, :, which, None] == slots[None, None, :]).astype(jnp.float32)
    agg = (
        jnp.einsum(
            "ekj,ejf->ekf", tally.astype(jnp.bfloat16), table, preferred_element_type=jnp.float32
        )
        / degree
    ).astype(jnp.bfloat16)
    zval = jnp.einsum("ekf,fh->ekh", pooled, w_self, preferred_element_type=jnp.float32)
    zval = zval + jnp.einsum("ekf,fh->ekh", agg, w_nbr, preferred_element_type=jnp.float32)
    sig = jax.nn.sigmoid(zval)
    units = (zval * sig).astype(jnp.bfloat16)
    scores = jnp.einsum("ekh,hc->ekc", units, w_out, preferred_element_type=jnp.float32)
    events = lax.axis_size("dp") * cells.shape[0]
    classes = jnp.arange(w_out.shape[1], dtype=jnp.int32)
    target = (labels[..., None] == classes[None, None, :]).astype(jnp.float32)
    d_logits = ((jax.nn.sigmoid(scores) - target) / events).astype(jnp.bfloat16)
    grad_head = jnp.einsum("ekh,ekc->hc", units, d_logits, preferred_element_type=jnp.float32)
    d_units = jnp.einsum("ekc,hc->ekh", d_logits, w_out, preferred_element_type=jnp.float32)
    d_z = (d_units * sig * (1.0 + zval * (1.0 - sig))).astype(jnp.bfloat16)
    grad_own = jnp.einsum("ekf,ekh->fh", pooled, d_z, preferred_element_type=jnp.float32)
    grad_side = jnp.einsum("ekf,ekh->fh", agg, d_z, preferred_element_type=jnp.float32)
    sizes = {"region": lax.axis_size("region"), "dp": lax.axis_size("dp")}
    feats, hid = grad_own.shape
    rows = 2 * feats
    head = grad_head.reshape(rows, -1)
    lanes = 128
    spare = jnp.zeros((rows, lanes - head.shape[1]), jnp.float32)
    packed = jnp.concatenate(
        [jnp.concatenate([grad_own, grad_side], axis=0), head, spare], axis=1
    )
    packed = all_sum(packed, sizes, 4)
    packed = packed.astype(jnp.float32)
    grad_own, grad_side = packed[:feats, :hid], packed[feats:, :hid]
    grad_head = packed[:, hid : hid + head.shape[1]].reshape(hid, -1)
    return (scores, grad_own, grad_side, grad_head)


def solution(mesh):
    return jax.shard_map(
        local,
        mesh=mesh,
        in_specs=(
            P("dp", "region", None),
            P("dp", "region"),
            P("dp", "region"),
            P("dp", "region", None),
            P("dp", "region"),
            P(),
            P(),
            P(),
        ),
        out_specs=(P("dp", "region", None), P(), P(), P()),
        check_vma=False,
    )
```

```python
import jax
import jax.numpy as jnp
from jax import lax
from jax.experimental import pallas as pl
from jax.sharding import PartitionSpec as P


def passed_along(value, axis, steps):
    count = lax.axis_size(axis)
    initial, last = (max(0, -steps), min(count, count - steps))
    return lax.ppermute(value, axis, [(source, source + steps) for source in range(initial, last)])


def padded(block, sides, width):
    for axis, dim in sides:
        count = lax.axis_size(axis)
        forward = [(i, i + 1) for i in range(count - 1)]
        backward = [(target, source) for source, target in forward]
        low = lax.ppermute(
            lax.slice_in_dim(block, block.shape[dim] - width, None, axis=dim), axis, forward
        )
        high = lax.ppermute(lax.slice_in_dim(block, 0, width, axis=dim), axis, backward)
        block = jnp.concatenate([low, block, high], axis=dim)
    return block


def pooled_sums_kernel(offset_ref, ids_ref, weight_ref, cells_ref, sums_ref):
    @pl.when(pl.program_id(0) == 0)
    def _():
        sums_ref[...] = jnp.zeros_like(sums_ref)

    width = sums_ref.shape[0]
    block = ids_ref.shape[1]
    feats = cells_ref.shape[1]
    lanes = sums_ref.shape[1] - feats
    ids = ids_ref[...] - offset_ref[0:1, 0:1]
    slots = lax.broadcasted_iota(jnp.int32, (width, block), 0)
    member = (ids == slots).astype(jnp.bfloat16)
    weight = weight_ref[...]
    high = weight.astype(jnp.bfloat16).astype(jnp.float32)
    rest = weight - high
    middle = rest.astype(jnp.bfloat16).astype(jnp.float32)
    low = rest - middle
    pad = jnp.zeros((lanes - 4, block), jnp.float32)
    columns = jnp.concatenate([high, middle, low, weight, pad], axis=0).T
    lane = lax.broadcasted_iota(jnp.int32, (block, lanes), 1)
    parts = jnp.where(lane < 3, columns, 0.0).astype(jnp.bfloat16)
    weighted = (columns[:, 3:4] * cells_ref[...].astype(jnp.float32)).astype(jnp.bfloat16)
    sums_ref[:, :feats] += jnp.dot(member, weighted, preferred_element_type=jnp.float32)
    sums_ref[:, feats:] += jnp.dot(member, parts, preferred_element_type=jnp.float32)


def accumulate(offset, cluster_ids, cells, weights, width):
    length, feats = cells.shape
    block = min(2048, length)
    lanes = 128
    offsets = jnp.full((8, lanes), offset, jnp.int32)
    sums = pl.pallas_call(
        pooled_sums_kernel,
        grid=(length // block,),
        in_specs=[
            pl.BlockSpec((8, lanes), lambda i: (0, 0)),
            pl.BlockSpec((1, block), lambda i: (0, i)),
            pl.BlockSpec((1, block), lambda i: (0, i)),
            pl.BlockSpec((block, feats), lambda i: (i, 0)),
        ],
        out_specs=pl.BlockSpec((width, feats + lanes), lambda i: (0, 0)),
        out_shape=jax.ShapeDtypeStruct((width, feats + lanes), jnp.float32),
        cost_estimate=pl.CostEstimate(
            flops=2 * width * length * (feats + lanes),
            bytes_accessed=length * (feats * 2 + 8) + width * (feats + lanes) * 4,
            transcendentals=0,
        ),
    )(offsets, cluster_ids.reshape(1, length), weights.reshape(1, length), cells)
    return sums


def halving_plan(sizes):
    core = [("region", 1)]
    first = [("region", 2), ("dp", 8), ("dp", 1), ("region", 4), ("dp", 16), ("dp", 2), ("dp", 4)]
    second = [("dp", 8), ("dp", 1), ("region", 2), ("dp", 16), ("dp", 2), ("region", 4), ("dp", 4)]
    width = sizes["dp"]
    steps = []
    for flip0, flip1 in zip(core + first, core + second):
        perm = []
        for device in range(sizes["region"] * width):
            at = {"region": device // width, "dp": device % width}
            axis, bit = flip1 if at["region"] & 1 else flip0
            at[axis] ^= bit
            perm.append((device, at["region"] * width + at["dp"]))
        steps.append((perm, flip0, flip1))
    return steps


def upper_half(flip0, flip1):
    core = lax.axis_index("region") % 2
    bit0 = (lax.axis_index(flip0[0]) // flip0[1]) % 2
    bit1 = (lax.axis_index(flip1[0]) // flip1[1]) % 2
    return jnp.where(core == 1, bit1, bit0) == 1


def all_sum(value, sizes, halvings):
    axes = ("region", "dp")
    steps = halving_plan(sizes)
    for perm, flip0, flip1 in steps[:halvings]:
        upper = upper_half(flip0, flip1)
        half = value.shape[0] // 2
        low, high = value[:half], value[half:]
        got = lax.ppermute(jnp.where(upper, low, high), axes, perm)
        value = jnp.where(upper, high, low) + got
    for perm, _, _ in steps[halvings:]:
        value = value + lax.ppermute(value, axes, perm)
    value = value.astype(jnp.bfloat16)
    for perm, flip0, flip1 in reversed(steps[:halvings]):
        upper = upper_half(flip0, flip1)
        got = lax.ppermute(value, axes, perm)
        value = jnp.concatenate(
            [jnp.where(upper, got, value), jnp.where(upper, value, got)], axis=0
        )
    return value


def local(cells, cell_weight, cell_cluster, cluster_edges, labels, w_self, w_nbr, w_out):
    region = lax.axis_index("region")
    owned = cluster_edges.shape[1]
    degree = cluster_edges.shape[2]
    sums = accumulate((region - 1) * owned, cell_cluster[0], cells[0], cell_weight[0], 3 * owned)
    above = passed_along(sums[:owned], "region", -1)
    below = passed_along(sums[2 * owned :], "region", 1)
    total = (sums[owned : 2 * owned] + above + below)[None]
    feats = cells.shape[2]
    numer = total[..., :feats]
    denom = total[..., feats] + total[..., feats + 1] + total[..., feats + 2]
    pooled = (numer / denom[..., None]).astype(jnp.bfloat16)
    table = padded(pooled, (("region", 1),), owned)
    targets = cluster_edges - (region - 1) * owned
    width = 3 * owned
    slots = jnp.arange(width, dtype=jnp.int32)
    tally = jnp.zeros((pooled.shape[0], owned, width), jnp.float32)
    for which in range(degree):
        tally = tally + (targets[:, :, which, None] == slots[None, None, :]).astype(jnp.float32)
    agg = (
        jnp.einsum(
            "ekj,ejf->ekf", tally.astype(jnp.bfloat16), table, preferred_element_type=jnp.float32
        )
        / degree
    ).astype(jnp.bfloat16)
    zval = jnp.einsum("ekf,fh->ekh", pooled, w_self, preferred_element_type=jnp.float32)
    zval = zval + jnp.einsum("ekf,fh->ekh", agg, w_nbr, preferred_element_type=jnp.float32)
    sig = jax.nn.sigmoid(zval)
    units = (zval * sig).astype(jnp.bfloat16)
    scores = jnp.einsum("ekh,hc->ekc", units, w_out, preferred_element_type=jnp.float32)
    events = lax.axis_size("dp") * cells.shape[0]
    classes = jnp.arange(w_out.shape[1], dtype=jnp.int32)
    target = (labels[..., None] == classes[None, None, :]).astype(jnp.float32)
    d_logits = ((jax.nn.sigmoid(scores) - target) / events).astype(jnp.bfloat16)
    grad_head = jnp.einsum("ekh,ekc->hc", units, d_logits, preferred_element_type=jnp.float32)
    d_units = jnp.einsum("ekc,hc->ekh", d_logits, w_out, preferred_element_type=jnp.float32)
    d_z = (d_units * sig * (1.0 + zval * (1.0 - sig))).astype(jnp.bfloat16)
    grad_own = jnp.einsum("ekf,ekh->fh", pooled, d_z, preferred_element_type=jnp.float32)
    grad_side = jnp.einsum("ekf,ekh->fh", agg, d_z, preferred_element_type=jnp.float32)
    sizes = {"region": lax.axis_size("region"), "dp": lax.axis_size("dp")}
    feats, hid = grad_own.shape
    rows = 2 * feats
    head = grad_head.reshape(rows, -1)
    lanes = 128
    spare = jnp.zeros((rows, lanes - head.shape[1]), jnp.float32)
    packed = jnp.concatenate(
        [jnp.concatenate([grad_own, grad_side], axis=0), head, spare], axis=1
    )
    packed = all_sum(packed, sizes, 4)
    packed = packed.astype(jnp.float32)
    grad_own, grad_side = packed[:feats, :hid], packed[feats:, :hid]
    grad_head = packed[:, hid : hid + head.shape[1]].reshape(hid, -1)
    return (scores, grad_own, grad_side, grad_head)


def solution(mesh):
    return jax.shard_map(
        local,
        mesh=mesh,
        in_specs=(
            P("dp", "region", None),
            P("dp", "region"),
            P("dp", "region"),
            P("dp", "region", None),
            P("dp", "region"),
            P(),
            P(),
            P(),
        ),
        out_specs=(P("dp", "region", None), P(), P(), P()),
        check_vma=False,
    )
```

```python
import jax
import jax.numpy as jnp
from jax import lax
from jax.experimental import pallas as pl
from jax.sharding import PartitionSpec as P


def passed_along(value, axis, steps):
    count = lax.axis_size(axis)
    initial, last = (max(0, -steps), min(count, count - steps))
    return lax.ppermute(value, axis, [(source, source + steps) for source in range(initial, last)])


def padded(block, sides, width):
    for axis, dim in sides:
        count = lax.axis_size(axis)
        forward = [(i, i + 1) for i in range(count - 1)]
        backward = [(target, source) for source, target in forward]
        low = lax.ppermute(
            lax.slice_in_dim(block, block.shape[dim] - width, None, axis=dim), axis, forward
        )
        high = lax.ppermute(lax.slice_in_dim(block, 0, width, axis=dim), axis, backward)
        block = jnp.concatenate([low, block, high], axis=dim)
    return block


def pooled_sums_kernel(offset_ref, ids_ref, weight_ref, cells_ref, sums_ref):
    @pl.when(pl.program_id(0) == 0)
    def _():
        sums_ref[...] = jnp.zeros_like(sums_ref)

    width = sums_ref.shape[0]
    block = ids_ref.shape[1]
    feats = cells_ref.shape[1]
    lanes = sums_ref.shape[1] - feats
    ids = ids_ref[...] - offset_ref[0:1, 0:1]
    slots = lax.broadcasted_iota(jnp.int32, (width, block), 0)
    member = (ids == slots).astype(jnp.bfloat16)
    weight = weight_ref[...]
    high = weight.astype(jnp.bfloat16).astype(jnp.float32)
    rest = weight - high
    middle = rest.astype(jnp.bfloat16).astype(jnp.float32)
    low = rest - middle
    pad = jnp.zeros((lanes - 4, block), jnp.float32)
    columns = jnp.concatenate([high, middle, low, weight, pad], axis=0).T
    lane = lax.broadcasted_iota(jnp.int32, (block, lanes), 1)
    parts = jnp.where(lane < 3, columns, 0.0).astype(jnp.bfloat16)
    weighted = (columns[:, 3:4] * cells_ref[...].astype(jnp.float32)).astype(jnp.bfloat16)
    sums_ref[:, :feats] += jnp.dot(member, weighted, preferred_element_type=jnp.float32)
    sums_ref[:, feats:] += jnp.dot(member, parts, preferred_element_type=jnp.float32)


def accumulate(offset, cluster_ids, cells, weights, width):
    length, feats = cells.shape
    block = min(2048, length)
    lanes = 128
    offsets = jnp.full((8, lanes), offset, jnp.int32)
    sums = pl.pallas_call(
        pooled_sums_kernel,
        grid=(length // block,),
        in_specs=[
            pl.BlockSpec((8, lanes), lambda i: (0, 0)),
            pl.BlockSpec((1, block), lambda i: (0, i)),
            pl.BlockSpec((1, block), lambda i: (0, i)),
            pl.BlockSpec((block, feats), lambda i: (i, 0)),
        ],
        out_specs=pl.BlockSpec((width, feats + lanes), lambda i: (0, 0)),
        out_shape=jax.ShapeDtypeStruct((width, feats + lanes), jnp.float32),
        cost_estimate=pl.CostEstimate(
            flops=2 * width * length * (feats + lanes),
            bytes_accessed=length * (feats * 2 + 8) + width * (feats + lanes) * 4,
            transcendentals=0,
        ),
    )(offsets, cluster_ids.reshape(1, length), weights.reshape(1, length), cells)
    return sums


def halving_plan(sizes):
    core = [("region", 1)]
    first = [("region", 2), ("dp", 8), ("dp", 1), ("dp", 4), ("region", 4), ("dp", 16), ("dp", 2)]
    second = [("dp", 8), ("dp", 1), ("region", 2), ("dp", 4), ("dp", 16), ("dp", 2), ("region", 4)]
    width = sizes["dp"]
    steps = []
    for flip0, flip1 in zip(core + first, core + second):
        perm = []
        for device in range(sizes["region"] * width):
            at = {"region": device // width, "dp": device % width}
            axis, bit = flip1 if at["region"] & 1 else flip0
            at[axis] ^= bit
            perm.append((device, at["region"] * width + at["dp"]))
        steps.append((perm, flip0, flip1))
    return steps


def upper_half(flip0, flip1):
    core = lax.axis_index("region") % 2
    bit0 = (lax.axis_index(flip0[0]) // flip0[1]) % 2
    bit1 = (lax.axis_index(flip1[0]) // flip1[1]) % 2
    return jnp.where(core == 1, bit1, bit0) == 1


def all_sum(value, sizes, halvings):
    axes = ("region", "dp")
    steps = halving_plan(sizes)
    for perm, flip0, flip1 in steps[:halvings]:
        upper = upper_half(flip0, flip1)
        half = value.shape[0] // 2
        low, high = value[:half], value[half:]
        got = lax.ppermute(jnp.where(upper, low, high), axes, perm)
        value = jnp.where(upper, high, low) + got
    for perm, _, _ in steps[halvings:]:
        value = value + lax.ppermute(value, axes, perm)
    value = value.astype(jnp.bfloat16)
    for perm, flip0, flip1 in reversed(steps[:halvings]):
        upper = upper_half(flip0, flip1)
        got = lax.ppermute(value, axes, perm)
        value = jnp.concatenate(
            [jnp.where(upper, got, value), jnp.where(upper, value, got)], axis=0
        )
    return value


def local(cells, cell_weight, cell_cluster, cluster_edges, labels, w_self, w_nbr, w_out):
    region = lax.axis_index("region")
    owned = cluster_edges.shape[1]
    degree = cluster_edges.shape[2]
    sums = accumulate((region - 1) * owned, cell_cluster[0], cells[0], cell_weight[0], 3 * owned)
    above = passed_along(sums[:owned], "region", -1)
    below = passed_along(sums[2 * owned :], "region", 1)
    total = (sums[owned : 2 * owned] + above + below)[None]
    feats = cells.shape[2]
    numer = total[..., :feats]
    denom = total[..., feats] + total[..., feats + 1] + total[..., feats + 2]
    pooled = (numer / denom[..., None]).astype(jnp.bfloat16)
    table = padded(pooled, (("region", 1),), owned)
    targets = cluster_edges - (region - 1) * owned
    width = 3 * owned
    slots = jnp.arange(width, dtype=jnp.int32)
    tally = jnp.zeros((pooled.shape[0], owned, width), jnp.float32)
    for which in range(degree):
        tally = tally + (targets[:, :, which, None] == slots[None, None, :]).astype(jnp.float32)
    agg = (
        jnp.einsum(
            "ekj,ejf->ekf", tally.astype(jnp.bfloat16), table, preferred_element_type=jnp.float32
        )
        / degree
    ).astype(jnp.bfloat16)
    zval = jnp.einsum("ekf,fh->ekh", pooled, w_self, preferred_element_type=jnp.float32)
    zval = zval + jnp.einsum("ekf,fh->ekh", agg, w_nbr, preferred_element_type=jnp.float32)
    sig = jax.nn.sigmoid(zval)
    units = (zval * sig).astype(jnp.bfloat16)
    scores = jnp.einsum("ekh,hc->ekc", units, w_out, preferred_element_type=jnp.float32)
    events = lax.axis_size("dp") * cells.shape[0]
    classes = jnp.arange(w_out.shape[1], dtype=jnp.int32)
    target = (labels[..., None] == classes[None, None, :]).astype(jnp.float32)
    d_logits = ((jax.nn.sigmoid(scores) - target) / events).astype(jnp.bfloat16)
    grad_head = jnp.einsum("ekh,ekc->hc", units, d_logits, preferred_element_type=jnp.float32)
    d_units = jnp.einsum("ekc,hc->ekh", d_logits, w_out, preferred_element_type=jnp.float32)
    d_z = (d_units * sig * (1.0 + zval * (1.0 - sig))).astype(jnp.bfloat16)
    grad_own = jnp.einsum("ekf,ekh->fh", pooled, d_z, preferred_element_type=jnp.float32)
    grad_side = jnp.einsum("ekf,ekh->fh", agg, d_z, preferred_element_type=jnp.float32)
    sizes = {"region": lax.axis_size("region"), "dp": lax.axis_size("dp")}
    feats, hid = grad_own.shape
    rows = 2 * feats
    head = grad_head.reshape(rows, -1)
    lanes = 128
    spare = jnp.zeros((rows, lanes - head.shape[1]), jnp.float32)
    packed = jnp.concatenate(
        [jnp.concatenate([grad_own, grad_side], axis=0), head, spare], axis=1
    )
    packed = all_sum(packed, sizes, 5)
    packed = packed.astype(jnp.float32)
    grad_own, grad_side = packed[:feats, :hid], packed[feats:, :hid]
    grad_head = packed[:, hid : hid + head.shape[1]].reshape(hid, -1)
    return (scores, grad_own, grad_side, grad_head)


def solution(mesh):
    return jax.shard_map(
        local,
        mesh=mesh,
        in_specs=(
            P("dp", "region", None),
            P("dp", "region"),
            P("dp", "region"),
            P("dp", "region", None),
            P("dp", "region"),
            P(),
            P(),
            P(),
        ),
        out_specs=(P("dp", "region", None), P(), P(), P()),
        check_vma=False,
    )
```

```python
import jax
import jax.numpy as jnp
from jax import lax
from jax.experimental import pallas as pl
from jax.sharding import PartitionSpec as P


def passed_along(value, axis, steps):
    count = lax.axis_size(axis)
    initial, last = (max(0, -steps), min(count, count - steps))
    return lax.ppermute(value, axis, [(source, source + steps) for source in range(initial, last)])


def padded(block, sides, width):
    for axis, dim in sides:
        count = lax.axis_size(axis)
        forward = [(i, i + 1) for i in range(count - 1)]
        backward = [(target, source) for source, target in forward]
        low = lax.ppermute(
            lax.slice_in_dim(block, block.shape[dim] - width, None, axis=dim), axis, forward
        )
        high = lax.ppermute(lax.slice_in_dim(block, 0, width, axis=dim), axis, backward)
        block = jnp.concatenate([low, block, high], axis=dim)
    return block


def pooled_sums_kernel(offset_ref, ids_ref, weight_ref, cells_ref, sums_ref):
    @pl.when(pl.program_id(0) == 0)
    def _():
        sums_ref[...] = jnp.zeros_like(sums_ref)

    width = sums_ref.shape[0]
    block = ids_ref.shape[1]
    feats = cells_ref.shape[1]
    lanes = sums_ref.shape[1] - feats
    ids = ids_ref[...] - offset_ref[0:1, 0:1]
    slots = lax.broadcasted_iota(jnp.int32, (width, block), 0)
    member = (ids == slots).astype(jnp.bfloat16)
    weight = weight_ref[...]
    high = weight.astype(jnp.bfloat16).astype(jnp.float32)
    rest = weight - high
    middle = rest.astype(jnp.bfloat16).astype(jnp.float32)
    low = rest - middle
    pad = jnp.zeros((lanes - 4, block), jnp.float32)
    columns = jnp.concatenate([high, middle, low, weight, pad], axis=0).T
    lane = lax.broadcasted_iota(jnp.int32, (block, lanes), 1)
    parts = jnp.where(lane < 3, columns, 0.0).astype(jnp.bfloat16)
    weighted = (columns[:, 3:4] * cells_ref[...].astype(jnp.float32)).astype(jnp.bfloat16)
    sums_ref[:, :feats] += jnp.dot(member, weighted, preferred_element_type=jnp.float32)
    sums_ref[:, feats:] += jnp.dot(member, parts, preferred_element_type=jnp.float32)


def accumulate(offset, cluster_ids, cells, weights, width):
    length, feats = cells.shape
    block = min(4096, length)
    lanes = 128
    offsets = jnp.full((8, lanes), offset, jnp.int32)
    sums = pl.pallas_call(
        pooled_sums_kernel,
        grid=(length // block,),
        in_specs=[
            pl.BlockSpec((8, lanes), lambda i: (0, 0)),
            pl.BlockSpec((1, block), lambda i: (0, i)),
            pl.BlockSpec((1, block), lambda i: (0, i)),
            pl.BlockSpec((block, feats), lambda i: (i, 0)),
        ],
        out_specs=pl.BlockSpec((width, feats + lanes), lambda i: (0, 0)),
        out_shape=jax.ShapeDtypeStruct((width, feats + lanes), jnp.float32),
        cost_estimate=pl.CostEstimate(
            flops=2 * width * length * (feats + lanes),
            bytes_accessed=length * (feats * 2 + 8) + width * (feats + lanes) * 4,
            transcendentals=0,
        ),
    )(offsets, cluster_ids.reshape(1, length), weights.reshape(1, length), cells)
    return sums


def halving_plan(sizes):
    core = [("region", 1)]
    first = [("region", 2), ("dp", 8), ("dp", 1), ("region", 4), ("dp", 16), ("dp", 2), ("dp", 4)]
    second = [("dp", 8), ("dp", 1), ("region", 2), ("dp", 16), ("dp", 2), ("region", 4), ("dp", 4)]
    width = sizes["dp"]
    steps = []
    for flip0, flip1 in zip(core + first, core + second):
        perm = []
        for device in range(sizes["region"] * width):
            at = {"region": device // width, "dp": device % width}
            axis, bit = flip1 if at["region"] & 1 else flip0
            at[axis] ^= bit
            perm.append((device, at["region"] * width + at["dp"]))
        steps.append((perm, flip0, flip1))
    return steps


def upper_half(flip0, flip1):
    core = lax.axis_index("region") % 2
    bit0 = (lax.axis_index(flip0[0]) // flip0[1]) % 2
    bit1 = (lax.axis_index(flip1[0]) // flip1[1]) % 2
    return jnp.where(core == 1, bit1, bit0) == 1


def all_sum(value, sizes, halvings):
    axes = ("region", "dp")
    steps = halving_plan(sizes)
    for perm, flip0, flip1 in steps[:halvings]:
        upper = upper_half(flip0, flip1)
        half = value.shape[0] // 2
        low, high = value[:half], value[half:]
        got = lax.ppermute(jnp.where(upper, low, high), axes, perm)
        value = jnp.where(upper, high, low) + got
    for perm, _, _ in steps[halvings:]:
        value = value + lax.ppermute(value, axes, perm)
    value = value.astype(jnp.bfloat16)
    for perm, flip0, flip1 in reversed(steps[:halvings]):
        upper = upper_half(flip0, flip1)
        got = lax.ppermute(value, axes, perm)
        value = jnp.concatenate(
            [jnp.where(upper, got, value), jnp.where(upper, value, got)], axis=0
        )
    return value


def local(cells, cell_weight, cell_cluster, cluster_edges, labels, w_self, w_nbr, w_out):
    region = lax.axis_index("region")
    owned = cluster_edges.shape[1]
    degree = cluster_edges.shape[2]
    sums = accumulate((region - 1) * owned, cell_cluster[0], cells[0], cell_weight[0], 3 * owned)
    above = passed_along(sums[:owned], "region", -1)
    below = passed_along(sums[2 * owned :], "region", 1)
    total = (sums[owned : 2 * owned] + above + below)[None]
    feats = cells.shape[2]
    numer = total[..., :feats]
    denom = total[..., feats] + total[..., feats + 1] + total[..., feats + 2]
    pooled = (numer / denom[..., None]).astype(jnp.bfloat16)
    table = padded(pooled, (("region", 1),), owned)
    targets = cluster_edges - (region - 1) * owned
    width = 3 * owned
    slots = jnp.arange(width, dtype=jnp.int32)
    tally = jnp.zeros((pooled.shape[0], owned, width), jnp.float32)
    for which in range(degree):
        tally = tally + (targets[:, :, which, None] == slots[None, None, :]).astype(jnp.float32)
    agg = (
        jnp.einsum(
            "ekj,ejf->ekf", tally.astype(jnp.bfloat16), table, preferred_element_type=jnp.float32
        )
        / degree
    ).astype(jnp.bfloat16)
    zval = jnp.einsum("ekf,fh->ekh", pooled, w_self, preferred_element_type=jnp.float32)
    zval = zval + jnp.einsum("ekf,fh->ekh", agg, w_nbr, preferred_element_type=jnp.float32)
    sig = jax.nn.sigmoid(zval)
    units = (zval * sig).astype(jnp.bfloat16)
    scores = jnp.einsum("ekh,hc->ekc", units, w_out, preferred_element_type=jnp.float32)
    events = lax.axis_size("dp") * cells.shape[0]
    classes = jnp.arange(w_out.shape[1], dtype=jnp.int32)
    target = (labels[..., None] == classes[None, None, :]).astype(jnp.float32)
    d_logits = ((jax.nn.sigmoid(scores) - target) / events).astype(jnp.bfloat16)
    grad_head = jnp.einsum("ekh,ekc->hc", units, d_logits, preferred_element_type=jnp.float32)
    d_units = jnp.einsum("ekc,hc->ekh", d_logits, w_out, preferred_element_type=jnp.float32)
    d_z = (d_units * sig * (1.0 + zval * (1.0 - sig))).astype(jnp.bfloat16)
    grad_own = jnp.einsum("ekf,ekh->fh", pooled, d_z, preferred_element_type=jnp.float32)
    grad_side = jnp.einsum("ekf,ekh->fh", agg, d_z, preferred_element_type=jnp.float32)
    sizes = {"region": lax.axis_size("region"), "dp": lax.axis_size("dp")}
    feats, hid = grad_own.shape
    rows = 2 * feats
    head = grad_head.reshape(rows, -1)
    lanes = 128
    spare = jnp.zeros((rows, lanes - head.shape[1]), jnp.float32)
    packed = jnp.concatenate(
        [jnp.concatenate([grad_own, grad_side], axis=0), head, spare], axis=1
    )
    packed = all_sum(packed, sizes, 4)
    packed = packed.astype(jnp.float32)
    grad_own, grad_side = packed[:feats, :hid], packed[feats:, :hid]
    grad_head = packed[:, hid : hid + head.shape[1]].reshape(hid, -1)
    return (scores, grad_own, grad_side, grad_head)


def solution(mesh):
    return jax.shard_map(
        local,
        mesh=mesh,
        in_specs=(
            P("dp", "region", None),
            P("dp", "region"),
            P("dp", "region"),
            P("dp", "region", None),
            P("dp", "region"),
            P(),
            P(),
            P(),
        ),
        out_specs=(P("dp", "region", None), P(), P(), P()),
        check_vma=False,
    )
```

```python
import jax
import jax.numpy as jnp
from jax import lax
from jax.experimental import pallas as pl
from jax.sharding import PartitionSpec as P


def passed_along(value, axis, steps):
    count = lax.axis_size(axis)
    initial, last = (max(0, -steps), min(count, count - steps))
    return lax.ppermute(value, axis, [(source, source + steps) for source in range(initial, last)])


def padded(block, sides, width):
    for axis, dim in sides:
        count = lax.axis_size(axis)
        forward = [(i, i + 1) for i in range(count - 1)]
        backward = [(target, source) for source, target in forward]
        low = lax.ppermute(
            lax.slice_in_dim(block, block.shape[dim] - width, None, axis=dim), axis, forward
        )
        high = lax.ppermute(lax.slice_in_dim(block, 0, width, axis=dim), axis, backward)
        block = jnp.concatenate([low, block, high], axis=dim)
    return block


def pooled_sums_kernel(offset_ref, ids_ref, weight_ref, cells_ref, sums_ref):
    @pl.when(pl.program_id(0) == 0)
    def _():
        sums_ref[...] = jnp.zeros_like(sums_ref)

    width = sums_ref.shape[0]
    block = ids_ref.shape[1]
    feats = cells_ref.shape[1]
    lanes = sums_ref.shape[1] - feats
    ids = ids_ref[...] - offset_ref[0:1, 0:1]
    slots = lax.broadcasted_iota(jnp.int32, (width, block), 0)
    member = (ids == slots).astype(jnp.bfloat16)
    weight = weight_ref[...]
    high = weight.astype(jnp.bfloat16).astype(jnp.float32)
    rest = weight - high
    middle = rest.astype(jnp.bfloat16).astype(jnp.float32)
    low = rest - middle
    pad = jnp.zeros((lanes - 4, block), jnp.float32)
    columns = jnp.concatenate([high, middle, low, weight, pad], axis=0).T
    lane = lax.broadcasted_iota(jnp.int32, (block, lanes), 1)
    parts = jnp.where(lane < 3, columns, 0.0).astype(jnp.bfloat16)
    weighted = (columns[:, 3:4] * cells_ref[...].astype(jnp.float32)).astype(jnp.bfloat16)
    sums_ref[:, :feats] += jnp.dot(member, weighted, preferred_element_type=jnp.float32)
    sums_ref[:, feats:] += jnp.dot(member, parts, preferred_element_type=jnp.float32)


def accumulate(offset, cluster_ids, cells, weights, width):
    length, feats = cells.shape
    block = min(4096, length)
    lanes = 128
    offsets = jnp.full((8, lanes), offset, jnp.int32)
    sums = pl.pallas_call(
        pooled_sums_kernel,
        grid=(length // block,),
        in_specs=[
            pl.BlockSpec((8, lanes), lambda i: (0, 0)),
            pl.BlockSpec((1, block), lambda i: (0, i)),
            pl.BlockSpec((1, block), lambda i: (0, i)),
            pl.BlockSpec((block, feats), lambda i: (i, 0)),
        ],
        out_specs=pl.BlockSpec((width, feats + lanes), lambda i: (0, 0)),
        out_shape=jax.ShapeDtypeStruct((width, feats + lanes), jnp.float32),
        cost_estimate=pl.CostEstimate(
            flops=2 * width * length * (feats + lanes),
            bytes_accessed=length * (feats * 2 + 8) + width * (feats + lanes) * 4,
            transcendentals=0,
        ),
    )(offsets, cluster_ids.reshape(1, length), weights.reshape(1, length), cells)
    return sums


def halving_plan(sizes):
    core = [("region", 1)]
    first = [("region", 2), ("dp", 8), ("dp", 1), ("region", 4), ("dp", 16), ("dp", 2), ("dp", 4)]
    second = [("dp", 8), ("dp", 1), ("region", 2), ("dp", 16), ("dp", 2), ("region", 4), ("dp", 4)]
    width = sizes["dp"]
    steps = []
    for flip0, flip1 in zip(core + first, core + second):
        perm = []
        for device in range(sizes["region"] * width):
            at = {"region": device // width, "dp": device % width}
            axis, bit = flip1 if at["region"] & 1 else flip0
            at[axis] ^= bit
            perm.append((device, at["region"] * width + at["dp"]))
        steps.append((perm, flip0, flip1))
    return steps


def upper_half(flip0, flip1):
    core = lax.axis_index("region") % 2
    bit0 = (lax.axis_index(flip0[0]) // flip0[1]) % 2
    bit1 = (lax.axis_index(flip1[0]) // flip1[1]) % 2
    return jnp.where(core == 1, bit1, bit0) == 1


def all_sum(value, sizes, halvings):
    axes = ("region", "dp")
    steps = halving_plan(sizes)
    for perm, flip0, flip1 in steps[:halvings]:
        upper = upper_half(flip0, flip1)
        half = value.shape[0] // 2
        low, high = value[:half], value[half:]
        got = lax.ppermute(jnp.where(upper, low, high), axes, perm)
        value = jnp.where(upper, high, low) + got
    for perm, _, _ in steps[halvings:]:
        value = value + lax.ppermute(value, axes, perm)
    value = value.astype(jnp.bfloat16)
    for perm, flip0, flip1 in reversed(steps[:halvings]):
        upper = upper_half(flip0, flip1)
        got = lax.ppermute(value, axes, perm)
        value = jnp.concatenate(
            [jnp.where(upper, got, value), jnp.where(upper, value, got)], axis=0
        )
    return value


def local(cells, cell_weight, cell_cluster, cluster_edges, labels, w_self, w_nbr, w_out):
    region = lax.axis_index("region")
    owned = cluster_edges.shape[1]
    degree = cluster_edges.shape[2]
    sums = accumulate((region - 1) * owned, cell_cluster[0], cells[0], cell_weight[0], 3 * owned)
    above = passed_along(sums[:owned], "region", -1)
    below = passed_along(sums[2 * owned :], "region", 1)
    total = (sums[owned : 2 * owned] + above + below)[None]
    feats = cells.shape[2]
    numer = total[..., :feats]
    denom = total[..., feats] + total[..., feats + 1] + total[..., feats + 2]
    pooled = (numer / denom[..., None]).astype(jnp.bfloat16)
    table = padded(pooled, (("region", 1),), owned)
    targets = cluster_edges - (region - 1) * owned
    width = 3 * owned
    slots = jnp.arange(width, dtype=jnp.int32)
    tally = jnp.zeros((pooled.shape[0], owned, width), jnp.float32)
    for which in range(degree):
        tally = tally + (targets[:, :, which, None] == slots[None, None, :]).astype(jnp.float32)
    agg = (
        jnp.einsum(
            "ekj,ejf->ekf", tally.astype(jnp.bfloat16), table, preferred_element_type=jnp.float32
        )
        / degree
    ).astype(jnp.bfloat16)
    zval = jnp.einsum("ekf,fh->ekh", pooled, w_self, preferred_element_type=jnp.float32)
    zval = zval + jnp.einsum("ekf,fh->ekh", agg, w_nbr, preferred_element_type=jnp.float32)
    sig = jax.nn.sigmoid(zval)
    units = (zval * sig).astype(jnp.bfloat16)
    scores = jnp.einsum("ekh,hc->ekc", units, w_out, preferred_element_type=jnp.float32)
    events = lax.axis_size("dp") * cells.shape[0]
    classes = jnp.arange(w_out.shape[1], dtype=jnp.int32)
    target = (labels[..., None] == classes[None, None, :]).astype(jnp.float32)
    d_logits = ((jax.nn.sigmoid(scores) - target) / events).astype(jnp.bfloat16)
    grad_head = jnp.einsum("ekh,ekc->hc", units, d_logits, preferred_element_type=jnp.float32)
    d_units = jnp.einsum("ekc,hc->ekh", d_logits, w_out, preferred_element_type=jnp.float32)
    d_z = (d_units * sig * (1.0 + zval * (1.0 - sig))).astype(jnp.bfloat16)
    both = jnp.concatenate([pooled, agg], axis=2)
    grads = jnp.einsum("ekf,ekh->fh", both, d_z, preferred_element_type=jnp.float32)
    sizes = {"region": lax.axis_size("region"), "dp": lax.axis_size("dp")}
    rows, hid = grads.shape
    feats = rows // 2
    head = grad_head.reshape(rows, -1)
    lanes = 128
    spare = jnp.zeros((rows, lanes - head.shape[1]), jnp.float32)
    packed = jnp.concatenate(
        [grads, head, spare], axis=1
    )
    packed = all_sum(packed, sizes, 4)
    packed = packed.astype(jnp.float32)
    grad_own, grad_side = packed[:feats, :hid], packed[feats:, :hid]
    grad_head = packed[:, hid : hid + head.shape[1]].reshape(hid, -1)
    return (scores, grad_own, grad_side, grad_head)


def solution(mesh):
    return jax.shard_map(
        local,
        mesh=mesh,
        in_specs=(
            P("dp", "region", None),
            P("dp", "region"),
            P("dp", "region"),
            P("dp", "region", None),
            P("dp", "region"),
            P(),
            P(),
            P(),
        ),
        out_specs=(P("dp", "region", None), P(), P(), P()),
        check_vma=False,
    )
```
